512 devices in a mesh: gx: 32 (over y, x, core), gy: 16 (over z).
Axes of the slice: x: 4, y: 4, z: 16, core: 2. Of those that a mesh axis runs over, the one named last changes fastest.
Arguments:
- rhs_field: float32 [256, 512, 256], P('gx', 'gy'), may hold values from -50 to 50
- alpha_coef: float32 [256, 512, 256], P('gx', 'gy'), may hold values from 0.2 to 5
- beta_coef: float32 [256, 512, 256], P('gx', 'gy'), may hold values from 0.3 to 27
Outputs:
- solution: float32 [256, 512, 256], P('gx', 'gy')
The draws below stay inside these ranges and needn't reach their ends.
All inputs are finite; a program needn't handle non-finite values.
Results may differ from the reference program's by a relative error of at most 0.0001.
Values sent between devices are 32-bit elements; how exact they have to be, the bound alone decides.
No kernel may reach another device: no remote copies, remote signals or barrier semaphores. Data moves between devices by JAX's collectives and lax.ppermute only.
A program may use at most 128 MiB of HBM per device.

```python
import math
import jax
import jax.numpy as jnp

LEVELS = 4
PRE_STEPS = 3
POST_STEPS = 3
COARSE_STEPS = 8
NX = 256
NY = 512
NZ = 256


def draw_rhs_field(key, part):
    noise = 10.0 * jax.random.normal(key, (NX, NY, NZ), jnp.float32)
    return jnp.clip(noise, -50.0, 50.0)


def draw_beta_coef(key, part):
    unit = jax.random.uniform(key, (NX, NY, NZ), jnp.float32)
    base = 0.3 * jnp.exp(unit * math.log(10.0))
    xpos = jnp.arange(NX, dtype=jnp.float32) / max(NX - 1, 1)
    ramp = 1.0 + 2.0 * xpos
    return base * ramp[:, None, None]


def level_of(key, extent, cuts, low, largest):
    loudness, own = 1.0, jax.random.fold_in(key, 6)
    for axis_at, shards_of in cuts:
        heights = jnp.exp(jax.random.uniform(jax.random.fold_in(own, axis_at), (shards_of,), jnp.float32, low / len(cuts), largest / len(cuts)))
        loudness = loudness * jnp.repeat(heights, extent[axis_at] // shards_of).reshape([-1 if axis == axis_at else 1 for axis in range(len(extent))])
    return loudness


def setup_inputs(seed: int = 0) -> dict:
    streams_of = jax.random.split(jax.random.key(seed), 4)
    rhs_field = draw_rhs_field(jax.random.fold_in(streams_of[3], 71), 0)
    alpha_coef = jnp.clip(jnp.exp(math.log(5.0) - 3.218876 * jax.random.uniform(streams_of[1], (NX, NY, NZ), jnp.float32) ** level_of(streams_of[1], (NX, NY, NZ), ((0, 32), (1, 16)), -0.2, 0.2)), 0.2, 5.0)
    beta_coef = draw_beta_coef(jax.random.fold_in(streams_of[3], 71), 0)
    return dict(rhs_field=rhs_field, alpha_coef=alpha_coef, beta_coef=beta_coef)


HELM_SHIFT = 0.05
LOW_FRACTION = 0.1


def restrict(values):
    first, second, third = values.shape
    return values.reshape(first // 2, 2, second // 2, 2, third // 2, 2).mean(axis=(1, 3, 5))


def prolong(values):
    return jnp.repeat(jnp.repeat(jnp.repeat(values, 2, 0), 2, 1), 2, 2)


def zero_pad(values):
    return jnp.pad(values, 1)


def neighbours(padded):
    return [padded[2:, 1:-1, 1:-1], padded[:-2, 1:-1, 1:-1], padded[1:-1, 2:, 1:-1],
            padded[1:-1, :-2, 1:-1], padded[1:-1, 1:-1, 2:], padded[1:-1, 1:-1, :-2]]


def apply_op(u_padded, b_padded, alpha_level, inv_spacing):
    field = u_padded[1:-1, 1:-1, 1:-1]
    interior = b_padded[1:-1, 1:-1, 1:-1]
    summed = jnp.zeros_like(field)
    for near_u, near_b in zip(neighbours(u_padded), neighbours(b_padded)):
        summed = summed + (interior + near_b) * (field - near_u)
    return HELM_SHIFT * alpha_level * field + (0.5 * inv_spacing) * summed


def smooth(field, source, alpha_level, b_padded, inv_spacing, upper, sweeps, start_zero, padder):
    lower = LOW_FRACTION * upper
    middle = 0.5 * (upper + lower)
    half_width = 0.5 * (upper - lower)
    scaled = middle / half_width
    factor = 1.0 / scaled
    if start_zero:
        residual = source
    else:
        residual = source - apply_op(padder(field), b_padded, alpha_level, inv_spacing)
    direction = residual / middle
    field = direction if start_zero else field + direction
    for k in range(1, sweeps):
        residual = source - apply_op(padder(field), b_padded, alpha_level, inv_spacing)
        factor_new = 1.0 / (2.0 * scaled - factor)
        direction = factor_new * factor * direction + (2.0 * factor_new / half_width) * residual
        field = field + direction
        factor = factor_new
    return field


def reference(rhs_field, alpha_coef, beta_coef):
    alphas = [alpha_coef]
    betas = [beta_coef]
    for level_idx in range(1, LEVELS):
        alphas.append(restrict(alphas[-1]))
        betas.append(restrict(betas[-1]))
    uppers = [HELM_SHIFT * jnp.max(alphas[i]) + 12.0 * jnp.max(betas[i]) / 4.0 ** i for i in range(LEVELS)]
    b_pads = [zero_pad(b) for b in betas]
    sources = [rhs_field]
    fields = []
    for level_idx in range(LEVELS - 1):
        inv_spacing = 1.0 / 4.0 ** level_idx
        smoothed = smooth(jnp.zeros_like(sources[level_idx]), sources[level_idx], alphas[level_idx],
                          b_pads[level_idx], inv_spacing, uppers[level_idx], PRE_STEPS, True, zero_pad)
        residual = sources[level_idx] - apply_op(zero_pad(smoothed), b_pads[level_idx], alphas[level_idx], inv_spacing)
        sources.append(restrict(residual))
        fields.append(smoothed)
    last = LEVELS - 1
    coarse = smooth(jnp.zeros_like(sources[last]), sources[last], alphas[last], b_pads[last],
                    1.0 / 4.0 ** last, uppers[last], COARSE_STEPS, True, zero_pad)
    for level_idx in range(LEVELS - 2, -1, -1):
        smoothed = fields[level_idx] + prolong(coarse)
        coarse = smooth(smoothed, sources[level_idx], alphas[level_idx], b_pads[level_idx],
                        1.0 / 4.0 ** level_idx, uppers[level_idx], POST_STEPS, False, zero_pad)
    return coarse
```

```python
import jax
import jax.numpy as jnp
from jax import lax
from jax.sharding import PartitionSpec as P

LEVELS = 4
PRE_STEPS = 3
POST_STEPS = 3
COARSE_STEPS = 8


HELM_SHIFT = 0.05
LOW_FRACTION = 0.1


def exchange(x):
    halos = []
    for axis, dim in (("gx", 0), ("gy", 1)):
        peers = lax.axis_size(axis)
        length = x.shape[dim]
        up = [(i, i + 1) for i in range(peers - 1)]
        down = [(i + 1, i) for i in range(peers - 1)]
        last = lax.slice_in_dim(x, length - 1, length, axis=dim)
        first = lax.slice_in_dim(x, 0, 1, axis=dim)
        before = lax.ppermute(last, axis, up)
        after = lax.ppermute(first, axis, down)
        halos.append((before, after))
    return halos


def shifted(x, halos):
    (lo0, hi0), (lo1, hi1) = halos
    zero2 = jnp.zeros_like(x[:, :, :1])
    return [
        jnp.concatenate([x[1:], hi0], axis=0),
        jnp.concatenate([lo0, x[:-1]], axis=0),
        jnp.concatenate([x[:, 1:], hi1], axis=1),
        jnp.concatenate([lo1, x[:, :-1]], axis=1),
        jnp.concatenate([x[:, :, 1:], zero2], axis=2),
        jnp.concatenate([zero2, x[:, :, :-1]], axis=2),
    ]


def coef_sums(beta_level):
    near = shifted(beta_level, exchange(beta_level))
    return [beta_level + b for b in near]


def pool_matrix(n, dtype):
    rows = jnp.arange(n)[:, None] // 2
    cols = jnp.arange(n // 2)[None, :]
    return (rows == cols).astype(dtype)


def restrict(values):
    first, second, third = values.shape
    pairs = values.reshape(first // 2, 2, second, third)
    summed = pairs[:, 0] + pairs[:, 1]
    pool1 = pool_matrix(second, values.dtype)
    pool2 = pool_matrix(third, values.dtype)
    summed = jnp.einsum("ajk,jb->abk", summed, pool1, precision=lax.Precision.HIGHEST)
    summed = jnp.einsum("abk,kc->abc", summed, pool2, precision=lax.Precision.HIGHEST)
    return summed * 0.125


def prolong(values):
    return jnp.repeat(jnp.repeat(jnp.repeat(values, 2, 0), 2, 1), 2, 2)


def apply_op(field, sums, alpha_level, inv_spacing):
    summed = jnp.zeros_like(field)
    for near_u, near_b in zip(shifted(field, exchange(field)), sums):
        summed = summed + near_b * (field - near_u)
    return HELM_SHIFT * alpha_level * field + 0.5 * inv_spacing * summed


def smooth(field, source, alpha_level, sums, inv_spacing, upper, sweeps, start_zero):
    lower = LOW_FRACTION * upper
    middle = 0.5 * (upper + lower)
    half_width = 0.5 * (upper - lower)
    scaled = middle / half_width
    factor = 1.0 / scaled
    if start_zero:
        residual = source
    else:
        residual = source - apply_op(field, sums, alpha_level, inv_spacing)
    direction = residual / middle
    field = direction if start_zero else field + direction
    for k in range(1, sweeps):
        residual = source - apply_op(field, sums, alpha_level, inv_spacing)
        factor_new = 1.0 / (2.0 * scaled - factor)
        direction = factor_new * factor * direction + 2.0 * factor_new / half_width * residual
        field = field + direction
        factor = factor_new
    return field


def all_max(values):
    for axis in ("gx", "gy"):
        peers = lax.axis_size(axis)
        if peers & (peers - 1):
            values = lax.pmax(values, axis)
            continue
        step = 1
        while step < peers:
            pairs = [(i, i ^ step) for i in range(peers)]
            values = jnp.maximum(values, lax.ppermute(values, axis, pairs))
            step *= 2
    return values


def local(rhs_field, alpha_coef, beta_coef):
    alphas = [alpha_coef]
    betas = [beta_coef]
    for level_idx in range(1, LEVELS):
        alphas.append(restrict(alphas[-1]))
        betas.append(restrict(betas[-1]))
    maxima = jnp.stack([jnp.stack([jnp.max(alphas[i]), jnp.max(betas[i])]) for i in range(LEVELS)])
    maxima = all_max(maxima)
    uppers = [HELM_SHIFT * maxima[i, 0] + 12.0 * maxima[i, 1] / 4.0**i for i in range(LEVELS)]
    sums = [coef_sums(betas[i]) for i in range(LEVELS)]
    sources = [rhs_field]
    fields = []
    for level_idx in range(LEVELS - 1):
        inv_spacing = 1.0 / 4.0**level_idx
        smoothed = smooth(
            jnp.zeros_like(sources[level_idx]),
            sources[level_idx],
            alphas[level_idx],
            sums[level_idx],
            inv_spacing,
            uppers[level_idx],
            PRE_STEPS,
            True,
        )
        residual = sources[level_idx] - apply_op(
            smoothed, sums[level_idx], alphas[level_idx], inv_spacing
        )
        sources.append(restrict(residual))
        fields.append(smoothed)
    last = LEVELS - 1
    coarse = smooth(
        jnp.zeros_like(sources[last]),
        sources[last],
        alphas[last],
        sums[last],
        1.0 / 4.0**last,
        uppers[last],
        COARSE_STEPS,
        True,
    )
    for level_idx in range(LEVELS - 2, -1, -1):
        smoothed = fields[level_idx] + prolong(coarse)
        coarse = smooth(
            smoothed,
            sources[level_idx],
            alphas[level_idx],
            sums[level_idx],
            1.0 / 4.0**level_idx,
            uppers[level_idx],
            POST_STEPS,
            False,
        )
    return coarse


def solution(mesh):
    placed = (P("gx", "gy", None), P("gx", "gy", None), P("gx", "gy", None))
    return jax.shard_map(
        local, mesh=mesh, in_specs=placed, out_specs=P("gx", "gy", None), check_vma=False
    )
```

```python
import jax
import jax.numpy as jnp
from jax import lax
from jax.sharding import PartitionSpec as P

LEVELS = 4
PRE_STEPS = 3
POST_STEPS = 3
COARSE_STEPS = 8


HELM_SHIFT = 0.05
LOW_FRACTION = 0.1
HALO_DEPTH = 3


def extend(x, depth):
    dim0 = x.ndim - 3
    for axis, dim in (("gx", dim0), ("gy", dim0 + 1)):
        peers = lax.axis_size(axis)
        length = x.shape[dim]
        up = [(i, i + 1) for i in range(peers - 1)]
        down = [(i + 1, i) for i in range(peers - 1)]
        last = lax.slice_in_dim(x, length - depth, length, axis=dim)
        first = lax.slice_in_dim(x, 0, depth, axis=dim)
        before = lax.ppermute(last, axis, up)
        after = lax.ppermute(first, axis, down)
        x = jnp.concatenate([before, x, after], axis=dim)
    return x


def crop(x, k):
    if k == 0:
        return x
    return x[..., k:-k, k:-k, :]


def neighbours(u):
    centre = u[1:-1, 1:-1]
    zero = jnp.zeros_like(centre[:, :, :1])
    return centre, [
        u[2:, 1:-1],
        u[:-2, 1:-1],
        u[1:-1, 2:],
        u[1:-1, :-2],
        jnp.concatenate([centre[:, :, 1:], zero], axis=2),
        jnp.concatenate([zero, centre[:, :, :-1]], axis=2),
    ]


def pool_matrix(n, dtype):
    rows = jnp.arange(n)[:, None] // 2
    cols = jnp.arange(n // 2)[None, :]
    return (rows == cols).astype(dtype)


def restrict(values):
    first, second, third = values.shape
    pairs = values.reshape(first // 2, 2, second, third)
    summed = pairs[:, 0] + pairs[:, 1]
    pool1 = pool_matrix(second, values.dtype)
    pool2 = pool_matrix(third, values.dtype)
    summed = jnp.einsum("ajk,jb->abk", summed, pool1, precision=lax.Precision.HIGHEST)
    summed = jnp.einsum("abk,kc->abc", summed, pool2, precision=lax.Precision.HIGHEST)
    return summed * 0.125


def prolong(values):
    return jnp.repeat(jnp.repeat(jnp.repeat(values, 2, 0), 2, 1), 2, 2)


def inside_mask(shape, depth):
    n0, n1 = shape[0], shape[1]
    rows = lax.axis_index("gx") * n0 + jnp.arange(n0 + 2 * depth) - depth
    cols = lax.axis_index("gy") * n1 + jnp.arange(n1 + 2 * depth) - depth
    ok0 = (rows >= 0) & (rows < n0 * lax.axis_size("gx"))
    ok1 = (cols >= 0) & (cols < n1 * lax.axis_size("gy"))
    return ok0[:, None, None] & ok1[None, :, None]


class Level:
    def __init__(self, source, alpha, beta, inv_spacing, upper):
        n0, n1 = source.shape[0], source.shape[1]
        self.depth = min(HALO_DEPTH, n0, n1)
        stacked = extend(jnp.stack([source, beta, alpha]), self.depth)
        self.source = stacked[0]
        beta_ext = stacked[1]
        self.alpha = stacked[2]
        centre, near = neighbours(beta_ext)
        self.sums = [centre + b for b in near]
        self.mask = inside_mask(source.shape, self.depth)
        self.inv_spacing = inv_spacing
        self.upper = upper

    def apply(self, u, e):
        centre, near = neighbours(u)
        sums = [crop(s, self.depth - e) for s in self.sums]
        alpha = crop(self.alpha, self.depth - e + 1)
        summed = jnp.zeros_like(centre)
        for near_u, near_b in zip(near, sums):
            summed = summed + near_b * (centre - near_u)
        return HELM_SHIFT * alpha * centre + 0.5 * self.inv_spacing * summed

    def residual(self, u, e):
        out = e - 1
        r = crop(self.source, self.depth - out) - self.apply(u, e)
        if out > 0:
            r = jnp.where(crop(self.mask, self.depth - out), r, 0.0)
        return r


def smooth(level, field, sweeps, start_zero, tail):
    upper = level.upper
    lower = LOW_FRACTION * upper
    middle = 0.5 * (upper + lower)
    half_width = 0.5 * (upper - lower)
    scaled = middle / half_width
    factor = 1.0 / scaled
    remaining = sweeps - 1 + tail if start_zero else sweeps + tail
    if start_zero:
        e = level.depth
        direction = level.source / middle
        field = direction
    else:
        e = min(level.depth, remaining)
        field = extend(field, e)
        residual = level.residual(field, e)
        remaining -= 1
        e -= 1
        direction = residual / middle
        field = crop(field, 1) + direction
    for k in range(1, sweeps):
        if e == 0:
            e = min(level.depth, remaining)
            both = extend(jnp.stack([field, direction]), e)
            field, direction = both[0], both[1]
        residual = level.residual(field, e)
        remaining -= 1
        e -= 1
        factor_new = 1.0 / (2.0 * scaled - factor)
        direction = (
            factor_new * factor * crop(direction, 1) + 2.0 * factor_new / half_width * residual
        )
        field = crop(field, 1) + direction
        factor = factor_new
    return field, e


def to_depth_zero(field, e):
    return crop(field, e)


def all_max(values):
    for axis in ("gx", "gy"):
        peers = lax.axis_size(axis)
        if peers & (peers - 1):
            values = lax.pmax(values, axis)
            continue
        step = 1
        while step < peers:
            pairs = [(i, i ^ step) for i in range(peers)]
            values = jnp.maximum(values, lax.ppermute(values, axis, pairs))
            step *= 2
    return values


def local(rhs_field, alpha_coef, beta_coef):
    alphas = [alpha_coef]
    betas = [beta_coef]
    for level_idx in range(1, LEVELS):
        alphas.append(restrict(alphas[-1]))
        betas.append(restrict(betas[-1]))
    maxima = jnp.stack([jnp.stack([jnp.max(alphas[i]), jnp.max(betas[i])]) for i in range(LEVELS)])
    maxima = all_max(maxima)
    uppers = [HELM_SHIFT * maxima[i, 0] + 12.0 * maxima[i, 1] / 4.0**i for i in range(LEVELS)]
    levels = []
    fields = []
    source = rhs_field
    for level_idx in range(LEVELS - 1):
        level = Level(source, alphas[level_idx], betas[level_idx], 1.0 / 4.0**level_idx, uppers[level_idx])
        levels.append(level)
        smoothed, e = smooth(level, None, PRE_STEPS, True, 1)
        if e == 0:
            e = 1
            smoothed_ext = extend(smoothed, 1)
        else:
            smoothed_ext = smoothed
        residual = level.residual(smoothed_ext, e)
        source = restrict(to_depth_zero(residual, e - 1))
        fields.append(to_depth_zero(smoothed_ext, e))
    last = LEVELS - 1
    level = Level(source, alphas[last], betas[last], 1.0 / 4.0**last, uppers[last])
    coarse, e = smooth(level, None, COARSE_STEPS, True, 0)
    coarse = to_depth_zero(coarse, e)
    for level_idx in range(LEVELS - 2, -1, -1):
        smoothed = fields[level_idx] + prolong(coarse)
        coarse, e = smooth(levels[level_idx], smoothed, POST_STEPS, False, 0)
        coarse = to_depth_zero(coarse, e)
    return coarse


def solution(mesh):
    placed = (P("gx", "gy", None), P("gx", "gy", None), P("gx", "gy", None))
    return jax.shard_map(
        local, mesh=mesh, in_specs=placed, out_specs=P("gx", "gy", None), check_vma=False
    )
```

```python
import jax
import jax.numpy as jnp
from jax import lax
from jax.sharding import PartitionSpec as P

LEVELS = 4
PRE_STEPS = 3
POST_STEPS = 3
COARSE_STEPS = 8


HELM_SHIFT = 0.05
LOW_FRACTION = 0.1


def halo_plan(size, depth):
    plan, held = [], 0
    while held < depth:
        take = min(depth - held, (1 + (2 * held) // size) * size)
        hop = -(-take // size)
        plan.append((held, take, hop))
        held += take
    return plan


def join(before, x, after, dim):
    if dim < x.ndim - 2:
        return jnp.concatenate([before, x, after], axis=dim)
    wide = before.shape[dim] + x.shape[dim] + after.shape[dim]

    def place(piece, at):
        pads = [(0, 0, 0)] * x.ndim
        pads[dim] = (at, wide - at - piece.shape[dim], 0)
        return lax.pad(piece, jnp.zeros((), piece.dtype), pads)

    return (
        place(before, 0)
        + place(x, before.shape[dim])
        + place(after, before.shape[dim] + x.shape[dim])
    )


def extend(x, depth):
    dim0 = x.ndim - 3
    for axis, dim in (("gx", dim0), ("gy", dim0 + 1)):
        peers = lax.axis_size(axis)
        size = x.shape[dim]
        plan = halo_plan(size, depth)
        cyclic = any(hop > 1 for _, _, hop in plan)
        for held, take, hop in plan:
            low = lax.slice_in_dim(x, hop * size - take, hop * size, axis=dim)
            start = size + 2 * held - hop * size
            high = lax.slice_in_dim(x, start, start + take, axis=dim)
            if cyclic:
                up = [(i, (i + hop) % peers) for i in range(peers)]
                down = [(i, (i - hop) % peers) for i in range(peers)]
            else:
                up = [(i, i + hop) for i in range(peers - hop)]
                down = [(i + hop, i) for i in range(peers - hop)]
            before = lax.ppermute(low, axis, up)
            after = lax.ppermute(high, axis, down)
            x = join(before, x, after, dim)
        if cyclic:
            index = lax.axis_index(axis) * size + jnp.arange(size + 2 * depth) - depth
            keep = (index >= 0) & (index < size * peers)
            keep = keep.reshape([-1 if d == dim else 1 for d in range(x.ndim)])
            x = jnp.where(keep, x, jnp.zeros_like(x))
    return x


def crop(x, k):
    if k == 0:
        return x
    return x[..., k:-k, k:-k, :]


def neighbours(u):
    centre = u[1:-1, 1:-1]
    zero = jnp.zeros_like(centre[:, :, :1])
    return centre, [
        u[2:, 1:-1],
        u[:-2, 1:-1],
        u[1:-1, 2:],
        u[1:-1, :-2],
        jnp.concatenate([centre[:, :, 1:], zero], axis=2),
        jnp.concatenate([zero, centre[:, :, :-1]], axis=2),
    ]


def pool_matrix(n, dtype):
    rows = jnp.arange(n)[:, None] // 2
    cols = jnp.arange(n // 2)[None, :]
    return (rows == cols).astype(dtype)


def restrict(values):
    first, second, third = values.shape
    pairs = values.reshape(first // 2, 2, second, third)
    summed = pairs[:, 0] + pairs[:, 1]
    pool1 = pool_matrix(second, values.dtype)
    pool2 = pool_matrix(third, values.dtype)
    summed = jnp.einsum("ajk,jb->abk", summed, pool1, precision=lax.Precision.HIGHEST)
    summed = jnp.einsum("abk,kc->abc", summed, pool2, precision=lax.Precision.HIGHEST)
    return summed * 0.125


def prolong(values):
    first, second, third = values.shape
    doubled = jnp.broadcast_to(values[:, None], (first, 2, second, third))
    doubled = doubled.reshape(2 * first, second, third)
    spread1 = pool_matrix(2 * second, values.dtype).T
    spread2 = pool_matrix(2 * third, values.dtype).T
    doubled = jnp.einsum("ajk,jb->abk", doubled, spread1, precision=lax.Precision.HIGHEST)
    return jnp.einsum("abk,kc->abc", doubled, spread2, precision=lax.Precision.HIGHEST)


def inside_mask(shape, depth):
    n0, n1 = shape[0], shape[1]
    rows = lax.axis_index("gx") * n0 + jnp.arange(n0 + 2 * depth) - depth
    cols = lax.axis_index("gy") * n1 + jnp.arange(n1 + 2 * depth) - depth
    ok0 = (rows >= 0) & (rows < n0 * lax.axis_size("gx"))
    ok1 = (cols >= 0) & (cols < n1 * lax.axis_size("gy"))
    return ok0[:, None, None] & ok1[None, :, None]


class Level:
    def __init__(self, source, alpha, beta, inv_spacing, upper, depth):
        self.depth = depth
        stacked = extend(jnp.stack([source, beta, alpha]), self.depth)
        self.source = stacked[0]
        beta_ext = stacked[1]
        self.alpha = stacked[2]
        centre, near = neighbours(beta_ext)
        self.sums = [centre + b for b in near]
        self.mask = inside_mask(source.shape, self.depth)
        self.inv_spacing = inv_spacing
        self.upper = upper

    def apply(self, u, e):
        centre, near = neighbours(u)
        sums = [crop(s, self.depth - e) for s in self.sums]
        alpha = crop(self.alpha, self.depth - e + 1)
        summed = jnp.zeros_like(centre)
        for near_u, near_b in zip(near, sums):
            summed = summed + near_b * (centre - near_u)
        return HELM_SHIFT * alpha * centre + 0.5 * self.inv_spacing * summed

    def residual(self, u, e):
        out = e - 1
        r = crop(self.source, self.depth - out) - self.apply(u, e)
        if out > 0:
            r = jnp.where(crop(self.mask, self.depth - out), r, 0.0)
        return r


def smooth(level, field, e, sweeps, start_zero):
    upper = level.upper
    lower = LOW_FRACTION * upper
    middle = 0.5 * (upper + lower)
    half_width = 0.5 * (upper - lower)
    scaled = middle / half_width
    factor = 1.0 / scaled
    if start_zero:
        e = level.depth
        direction = level.source / middle
        field = direction
    else:
        residual = level.residual(field, e)
        e -= 1
        direction = residual / middle
        field = crop(field, 1) + direction
    for k in range(1, sweeps):
        residual = level.residual(field, e)
        e -= 1
        factor_new = 1.0 / (2.0 * scaled - factor)
        direction = (
            factor_new * factor * crop(direction, 1) + 2.0 * factor_new / half_width * residual
        )
        field = crop(field, 1) + direction
        factor = factor_new
    return field, e


def all_max(values):
    for axis in ("gx", "gy"):
        peers = lax.axis_size(axis)
        if peers & (peers - 1):
            values = lax.pmax(values, axis)
            continue
        step = 1
        while step < peers:
            pairs = [(i, i ^ step) for i in range(peers)]
            values = jnp.maximum(values, lax.ppermute(values, axis, pairs))
            step *= 2
    return values


def local(rhs_field, alpha_coef, beta_coef):
    alphas = [alpha_coef]
    betas = [beta_coef]
    for level_idx in range(1, LEVELS):
        alphas.append(restrict(alphas[-1]))
        betas.append(restrict(betas[-1]))
    maxima = jnp.stack([jnp.stack([jnp.max(alphas[i]), jnp.max(betas[i])]) for i in range(LEVELS)])
    maxima = all_max(maxima)
    uppers = [HELM_SHIFT * maxima[i, 0] + 12.0 * maxima[i, 1] / 4.0**i for i in range(LEVELS)]
    out_depth = [0]
    for level_idx in range(1, LEVELS):
        out_depth.append(-(-(out_depth[-1] + POST_STEPS) // 2))
    depths = [out_depth[i] + POST_STEPS + PRE_STEPS - 1 for i in range(LEVELS - 1)]
    depths.append(out_depth[LEVELS - 1] + COARSE_STEPS - 1)
    levels = []
    fields = []
    source = rhs_field
    for level_idx in range(LEVELS - 1):
        level = Level(
            source,
            alphas[level_idx],
            betas[level_idx],
            1.0 / 4.0**level_idx,
            uppers[level_idx],
            depths[level_idx],
        )
        levels.append(level)
        smoothed, e = smooth(level, None, 0, PRE_STEPS, True)
        residual = level.residual(smoothed, e)
        source = restrict(crop(residual, e - 1))
        fields.append((smoothed, e))
    last = LEVELS - 1
    level = Level(source, alphas[last], betas[last], 1.0 / 4.0**last, uppers[last], depths[last])
    coarse, e = smooth(level, None, 0, COARSE_STEPS, True)
    for level_idx in range(LEVELS - 2, -1, -1):
        smoothed, have = fields[level_idx]
        need = out_depth[level_idx] + POST_STEPS
        correction = crop(prolong(coarse), 2 * e - need)
        coarse, e = smooth(
            levels[level_idx], crop(smoothed, have - need) + correction, need, POST_STEPS, False
        )
    return crop(coarse, e)


def solution(mesh):
    placed = (P("gx", "gy", None), P("gx", "gy", None), P("gx", "gy", None))
    return jax.shard_map(
        local, mesh=mesh, in_specs=placed, out_specs=P("gx", "gy", None), check_vma=False
    )
```

```python
import jax
import jax.numpy as jnp
from jax import lax
from jax.sharding import PartitionSpec as P

LEVELS = 4
PRE_STEPS = 3
POST_STEPS = 3
COARSE_STEPS = 8


HELM_SHIFT = 0.05
LOW_FRACTION = 0.1


def halo_plan(size, depth):
    plan, held = [], 0
    while held < depth:
        take = min(depth - held, (1 + (2 * held) // size) * size)
        hop = -(-take // size)
        plan.append((held, take, hop))
        held += take
    return plan


def join(before, x, after, dim):
    if dim < x.ndim - 2:
        return jnp.concatenate([before, x, after], axis=dim)
    wide = before.shape[dim] + x.shape[dim] + after.shape[dim]

    def place(piece, at):
        pads = [(0, 0, 0)] * x.ndim
        pads[dim] = (at, wide - at - piece.shape[dim], 0)
        return lax.pad(piece, jnp.zeros((), piece.dtype), pads)

    return (
        place(before, 0)
        + place(x, before.shape[dim])
        + place(after, before.shape[dim] + x.shape[dim])
    )


def extend(x, depth):
    dim0 = x.ndim - 3
    for axis, dim in (("gx", dim0), ("gy", dim0 + 1)):
        peers = lax.axis_size(axis)
        size = x.shape[dim]
        plan = halo_plan(size, depth)
        if len(plan) > 2:
            whole = lax.all_gather(x, axis, axis=dim, tiled=True)
            pads = [(0, 0, 0)] * x.ndim
            pads[dim] = (depth, depth, 0)
            whole = lax.pad(whole, jnp.zeros((), x.dtype), pads)
            x = lax.dynamic_slice_in_dim(
                whole, lax.axis_index(axis) * size, size + 2 * depth, axis=dim
            )
            continue
        cyclic = any(hop > 1 for _, _, hop in plan)
        for held, take, hop in plan:
            low = lax.slice_in_dim(x, hop * size - take, hop * size, axis=dim)
            start = size + 2 * held - hop * size
            high = lax.slice_in_dim(x, start, start + take, axis=dim)
            if cyclic:
                up = [(i, (i + hop) % peers) for i in range(peers)]
                down = [(i, (i - hop) % peers) for i in range(peers)]
            else:
                up = [(i, i + hop) for i in range(peers - hop)]
                down = [(i + hop, i) for i in range(peers - hop)]
            before = lax.ppermute(low, axis, up)
            after = lax.ppermute(high, axis, down)
            x = join(before, x, after, dim)
        if cyclic:
            index = lax.axis_index(axis) * size + jnp.arange(size + 2 * depth) - depth
            keep = (index >= 0) & (index < size * peers)
            keep = keep.reshape([-1 if d == dim else 1 for d in range(x.ndim)])
            x = jnp.where(keep, x, jnp.zeros_like(x))
    return x


def crop(x, k):
    if k == 0:
        return x
    return x[..., k:-k, k:-k, :]


def neighbours(u):
    centre = u[1:-1, 1:-1]
    zero = jnp.zeros_like(centre[:, :, :1])
    return centre, [
        u[2:, 1:-1],
        u[:-2, 1:-1],
        u[1:-1, 2:],
        u[1:-1, :-2],
        jnp.concatenate([centre[:, :, 1:], zero], axis=2),
        jnp.concatenate([zero, centre[:, :, :-1]], axis=2),
    ]


def pool_matrix(n, dtype):
    rows = jnp.arange(n)[:, None] // 2
    cols = jnp.arange(n // 2)[None, :]
    return (rows == cols).astype(dtype)


def restrict(values):
    first, second, third = values.shape
    pairs = values.reshape(first // 2, 2, second, third)
    summed = pairs[:, 0] + pairs[:, 1]
    pool1 = pool_matrix(second, values.dtype)
    pool2 = pool_matrix(third, values.dtype)
    summed = jnp.einsum("ajk,jb->abk", summed, pool1, precision=lax.Precision.HIGHEST)
    summed = jnp.einsum("abk,kc->abc", summed, pool2, precision=lax.Precision.HIGHEST)
    return summed * 0.125


def prolong(values):
    first, second, third = values.shape
    doubled = jnp.broadcast_to(values[:, None], (first, 2, second, third))
    doubled = doubled.reshape(2 * first, second, third)
    spread1 = pool_matrix(2 * second, values.dtype).T
    spread2 = pool_matrix(2 * third, values.dtype).T
    doubled = jnp.einsum("ajk,jb->abk", doubled, spread1, precision=lax.Precision.HIGHEST)
    return jnp.einsum("abk,kc->abc", doubled, spread2, precision=lax.Precision.HIGHEST)


def inside_mask(shape, depth):
    n0, n1 = shape[0], shape[1]
    rows = lax.axis_index("gx") * n0 + jnp.arange(n0 + 2 * depth) - depth
    cols = lax.axis_index("gy") * n1 + jnp.arange(n1 + 2 * depth) - depth
    ok0 = (rows >= 0) & (rows < n0 * lax.axis_size("gx"))
    ok1 = (cols >= 0) & (cols < n1 * lax.axis_size("gy"))
    return ok0[:, None, None] & ok1[None, :, None]


class Level:
    def __init__(self, source, alpha, beta, inv_spacing, upper, depth):
        self.depth = depth
        stacked = extend(jnp.stack([source, beta, alpha]), self.depth)
        self.source = stacked[0]
        beta_ext = stacked[1]
        self.alpha = stacked[2]
        centre, near = neighbours(beta_ext)
        self.sums = [centre + b for b in near]
        self.mask = inside_mask(source.shape, self.depth)
        self.inv_spacing = inv_spacing
        self.upper = upper

    def apply(self, u, e):
        centre, near = neighbours(u)
        sums = [crop(s, self.depth - e) for s in self.sums]
        alpha = crop(self.alpha, self.depth - e + 1)
        summed = jnp.zeros_like(centre)
        for near_u, near_b in zip(near, sums):
            summed = summed + near_b * (centre - near_u)
        return HELM_SHIFT * alpha * centre + 0.5 * self.inv_spacing * summed

    def residual(self, u, e):
        out = e - 1
        r = crop(self.source, self.depth - out) - self.apply(u, e)
        if out > 0:
            r = jnp.where(crop(self.mask, self.depth - out), r, 0.0)
        return r


def smooth(level, field, e, sweeps, start_zero):
    upper = level.upper
    lower = LOW_FRACTION * upper
    middle = 0.5 * (upper + lower)
    half_width = 0.5 * (upper - lower)
    scaled = middle / half_width
    factor = 1.0 / scaled
    if start_zero:
        e = level.depth
        direction = level.source / middle
        field = direction
    else:
        residual = level.residual(field, e)
        e -= 1
        direction = residual / middle
        field = crop(field, 1) + direction
    for k in range(1, sweeps):
        residual = level.residual(field, e)
        e -= 1
        factor_new = 1.0 / (2.0 * scaled - factor)
        direction = (
            factor_new * factor * crop(direction, 1) + 2.0 * factor_new / half_width * residual
        )
        field = crop(field, 1) + direction
        factor = factor_new
    return field, e


def all_max(values):
    for axis in ("gx", "gy"):
        peers = lax.axis_size(axis)
        if peers & (peers - 1):
            values = lax.pmax(values, axis)
            continue
        step = 1
        while step < peers:
            pairs = [(i, i ^ step) for i in range(peers)]
            values = jnp.maximum(values, lax.ppermute(values, axis, pairs))
            step *= 2
    return values


def local(rhs_field, alpha_coef, beta_coef):
    alphas = [alpha_coef]
    betas = [beta_coef]
    for level_idx in range(1, LEVELS):
        alphas.append(restrict(alphas[-1]))
        betas.append(restrict(betas[-1]))
    maxima = jnp.stack([jnp.stack([jnp.max(alphas[i]), jnp.max(betas[i])]) for i in range(LEVELS)])
    maxima = all_max(maxima)
    uppers = [HELM_SHIFT * maxima[i, 0] + 12.0 * maxima[i, 1] / 4.0**i for i in range(LEVELS)]
    out_depth = [0]
    for level_idx in range(1, LEVELS):
        out_depth.append(-(-(out_depth[-1] + POST_STEPS) // 2))
    depths = [out_depth[i] + POST_STEPS + PRE_STEPS - 1 for i in range(LEVELS - 1)]
    depths.append(out_depth[LEVELS - 1] + COARSE_STEPS - 1)
    levels = []
    fields = []
    source = rhs_field
    for level_idx in range(LEVELS - 1):
        level = Level(
            source,
            alphas[level_idx],
            betas[level_idx],
            1.0 / 4.0**level_idx,
            uppers[level_idx],
            depths[level_idx],
        )
        levels.append(level)
        smoothed, e = smooth(level, None, 0, PRE_STEPS, True)
        residual = level.residual(smoothed, e)
        source = restrict(crop(residual, e - 1))
        fields.append((smoothed, e))
    last = LEVELS - 1
    level = Level(source, alphas[last], betas[last], 1.0 / 4.0**last, uppers[last], depths[last])
    coarse, e = smooth(level, None, 0, COARSE_STEPS, True)
    for level_idx in range(LEVELS - 2, -1, -1):
        smoothed, have = fields[level_idx]
        need = out_depth[level_idx] + POST_STEPS
        correction = crop(prolong(coarse), 2 * e - need)
        coarse, e = smooth(
            levels[level_idx], crop(smoothed, have - need) + correction, need, POST_STEPS, False
        )
    return crop(coarse, e)


def solution(mesh):
    placed = (P("gx", "gy", None), P("gx", "gy", None), P("gx", "gy", None))
    return jax.shard_map(
        local, mesh=mesh, in_specs=placed, out_specs=P("gx", "gy", None), check_vma=False
    )
```

```python
import jax
import jax.numpy as jnp
from jax import lax
from jax.sharding import PartitionSpec as P

LEVELS = 4
PRE_STEPS = 3
POST_STEPS = 3
COARSE_STEPS = 8


HELM_SHIFT = 0.05
LOW_FRACTION = 0.1


def halo_plan(size, depth):
    plan, held = [], 0
    while held < depth:
        take = min(depth - held, (1 + (2 * held) // size) * size)
        hop = -(-take // size)
        plan.append((held, take, hop))
        held += take
    return plan


def join(before, x, after, dim):
    if dim < x.ndim - 2:
        return jnp.concatenate([before, x, after], axis=dim)
    wide = before.shape[dim] + x.shape[dim] + after.shape[dim]

    def place(piece, at):
        pads = [(0, 0, 0)] * x.ndim
        pads[dim] = (at, wide - at - piece.shape[dim], 0)
        return lax.pad(piece, jnp.zeros((), piece.dtype), pads)

    return (
        place(before, 0)
        + place(x, before.shape[dim])
        + place(after, before.shape[dim] + x.shape[dim])
    )


def extend(x, depth, gather=False):
    dim0 = x.ndim - 3
    for axis, dim in (("gx", dim0), ("gy", dim0 + 1)):
        peers = lax.axis_size(axis)
        size = x.shape[dim]
        plan = halo_plan(size, depth)
        if gather or len(plan) > 2:
            whole = lax.all_gather(x, axis, axis=dim, tiled=True)
            pads = [(0, 0, 0)] * x.ndim
            pads[dim] = (depth, depth, 0)
            whole = lax.pad(whole, jnp.zeros((), x.dtype), pads)
            x = lax.dynamic_slice_in_dim(
                whole, lax.axis_index(axis) * size, size + 2 * depth, axis=dim
            )
            continue
        cyclic = any(hop > 1 for _, _, hop in plan)
        for held, take, hop in plan:
            low = lax.slice_in_dim(x, hop * size - take, hop * size, axis=dim)
            start = size + 2 * held - hop * size
            high = lax.slice_in_dim(x, start, start + take, axis=dim)
            if cyclic:
                up = [(i, (i + hop) % peers) for i in range(peers)]
                down = [(i, (i - hop) % peers) for i in range(peers)]
            else:
                up = [(i, i + hop) for i in range(peers - hop)]
                down = [(i + hop, i) for i in range(peers - hop)]
            before = lax.ppermute(low, axis, up)
            after = lax.ppermute(high, axis, down)
            x = join(before, x, after, dim)
        if cyclic:
            index = lax.axis_index(axis) * size + jnp.arange(size + 2 * depth) - depth
            keep = (index >= 0) & (index < size * peers)
            keep = keep.reshape([-1 if d == dim else 1 for d in range(x.ndim)])
            x = jnp.where(keep, x, jnp.zeros_like(x))
    return x


def crop(x, k):
    if k == 0:
        return x
    return x[..., k:-k, k:-k, :]


def neighbours(u):
    centre = u[1:-1, 1:-1]
    zero = jnp.zeros_like(centre[:, :, :1])
    return centre, [
        u[2:, 1:-1],
        u[:-2, 1:-1],
        u[1:-1, 2:],
        u[1:-1, :-2],
        jnp.concatenate([centre[:, :, 1:], zero], axis=2),
        jnp.concatenate([zero, centre[:, :, :-1]], axis=2),
    ]


def pool_matrix(n, dtype):
    rows = jnp.arange(n)[:, None] // 2
    cols = jnp.arange(n // 2)[None, :]
    return (rows == cols).astype(dtype)


def restrict(values):
    first, second, third = values.shape
    pairs = values.reshape(first // 2, 2, second, third)
    summed = pairs[:, 0] + pairs[:, 1]
    pool1 = pool_matrix(second, values.dtype)
    pool2 = pool_matrix(third, values.dtype)
    summed = jnp.einsum("ajk,jb->abk", summed, pool1, precision=lax.Precision.HIGHEST)
    summed = jnp.einsum("abk,kc->abc", summed, pool2, precision=lax.Precision.HIGHEST)
    return summed * 0.125


def prolong(values):
    first, second, third = values.shape
    doubled = jnp.broadcast_to(values[:, None], (first, 2, second, third))
    doubled = doubled.reshape(2 * first, second, third)
    spread1 = pool_matrix(2 * second, values.dtype).T
    spread2 = pool_matrix(2 * third, values.dtype).T
    doubled = jnp.einsum("ajk,jb->abk", doubled, spread1, precision=lax.Precision.HIGHEST)
    return jnp.einsum("abk,kc->abc", doubled, spread2, precision=lax.Precision.HIGHEST)


def inside_mask(shape, depth):
    n0, n1 = shape[0], shape[1]
    rows = lax.axis_index("gx") * n0 + jnp.arange(n0 + 2 * depth) - depth
    cols = lax.axis_index("gy") * n1 + jnp.arange(n1 + 2 * depth) - depth
    ok0 = (rows >= 0) & (rows < n0 * lax.axis_size("gx"))
    ok1 = (cols >= 0) & (cols < n1 * lax.axis_size("gy"))
    return ok0[:, None, None] & ok1[None, :, None]


class Level:
    def __init__(self, source, alpha, beta, inv_spacing, upper, depth, gather=False):
        self.depth = depth
        stacked = extend(jnp.stack([source, beta, alpha]), self.depth, gather)
        self.source = stacked[0]
        beta_ext = stacked[1]
        self.alpha = stacked[2]
        centre, near = neighbours(beta_ext)
        self.sums = [centre + b for b in near]
        self.mask = inside_mask(source.shape, self.depth)
        self.inv_spacing = inv_spacing
        self.upper = upper

    def apply(self, u, e):
        centre, near = neighbours(u)
        sums = [crop(s, self.depth - e) for s in self.sums]
        alpha = crop(self.alpha, self.depth - e + 1)
        summed = jnp.zeros_like(centre)
        for near_u, near_b in zip(near, sums):
            summed = summed + near_b * (centre - near_u)
        return HELM_SHIFT * alpha * centre + 0.5 * self.inv_spacing * summed

    def residual(self, u, e):
        out = e - 1
        r = crop(self.source, self.depth - out) - self.apply(u, e)
        if out > 0:
            r = jnp.where(crop(self.mask, self.depth - out), r, 0.0)
        return r


def smooth(level, field, e, sweeps, start_zero):
    upper = level.upper
    lower = LOW_FRACTION * upper
    middle = 0.5 * (upper + lower)
    half_width = 0.5 * (upper - lower)
    scaled = middle / half_width
    factor = 1.0 / scaled
    if start_zero:
        e = level.depth
        direction = level.source / middle
        field = direction
    else:
        residual = level.residual(field, e)
        e -= 1
        direction = residual / middle
        field = crop(field, 1) + direction
    for k in range(1, sweeps):
        residual = level.residual(field, e)
        e -= 1
        factor_new = 1.0 / (2.0 * scaled - factor)
        direction = (
            factor_new * factor * crop(direction, 1) + 2.0 * factor_new / half_width * residual
        )
        field = crop(field, 1) + direction
        factor = factor_new
    return field, e


def all_max(values):
    for axis in ("gx", "gy"):
        peers = lax.axis_size(axis)
        if peers & (peers - 1):
            values = lax.pmax(values, axis)
            continue
        step = 1
        while step < peers:
            pairs = [(i, i ^ step) for i in range(peers)]
            values = jnp.maximum(values, lax.ppermute(values, axis, pairs))
            step *= 2
    return values


def local(rhs_field, alpha_coef, beta_coef):
    alphas = [alpha_coef]
    betas = [beta_coef]
    for level_idx in range(1, LEVELS):
        alphas.append(restrict(alphas[-1]))
        betas.append(restrict(betas[-1]))
    maxima = jnp.stack([jnp.stack([jnp.max(alphas[i]), jnp.max(betas[i])]) for i in range(LEVELS)])
    maxima = all_max(maxima)
    uppers = [HELM_SHIFT * maxima[i, 0] + 12.0 * maxima[i, 1] / 4.0**i for i in range(LEVELS)]
    out_depth = [0]
    for level_idx in range(1, LEVELS):
        out_depth.append(-(-(out_depth[-1] + POST_STEPS) // 2))
    depths = [out_depth[i] + POST_STEPS + PRE_STEPS - 1 for i in range(LEVELS - 1)]
    depths.append(out_depth[LEVELS - 1] + COARSE_STEPS - 1)
    levels = []
    fields = []
    source = rhs_field
    for level_idx in range(LEVELS - 1):
        level = Level(
            source,
            alphas[level_idx],
            betas[level_idx],
            1.0 / 4.0**level_idx,
            uppers[level_idx],
            depths[level_idx],
        )
        levels.append(level)
        smoothed, e = smooth(level, None, 0, PRE_STEPS, True)
        residual = level.residual(smoothed, e)
        source = restrict(crop(residual, e - 1))
        fields.append((smoothed, e))
    last = LEVELS - 1
    level = Level(
        source, alphas[last], betas[last], 1.0 / 4.0**last, uppers[last], depths[last], True
    )
    coarse, e = smooth(level, None, 0, COARSE_STEPS, True)
    for level_idx in range(LEVELS - 2, -1, -1):
        smoothed, have = fields[level_idx]
        need = out_depth[level_idx] + POST_STEPS
        correction = crop(prolong(coarse), 2 * e - need)
        coarse, e = smooth(
            levels[level_idx], crop(smoothed, have - need) + correction, need, POST_STEPS, False
        )
    return crop(coarse, e)


def solution(mesh):
    placed = (P("gx", "gy", None), P("gx", "gy", None), P("gx", "gy", None))
    return jax.shard_map(
        local, mesh=mesh, in_specs=placed, out_specs=P("gx", "gy", None), check_vma=False
    )
```

```python
import jax
import jax.numpy as jnp
from jax import lax
from jax.sharding import PartitionSpec as P

LEVELS = 4
PRE_STEPS = 3
POST_STEPS = 3
COARSE_STEPS = 8


HELM_SHIFT = 0.05
LOW_FRACTION = 0.1


def halo_plan(size, depth):
    plan, held = [], 0
    while held < depth:
        take = min(depth - held, (1 + (2 * held) // size) * size)
        hop = -(-take // size)
        plan.append((held, take, hop))
        held += take
    return plan


def join(before, x, after, dim):
    if dim < x.ndim - 2:
        return jnp.concatenate([before, x, after], axis=dim)
    wide = before.shape[dim] + x.shape[dim] + after.shape[dim]

    def place(piece, at):
        pads = [(0, 0, 0)] * x.ndim
        pads[dim] = (at, wide - at - piece.shape[dim], 0)
        return lax.pad(piece, jnp.zeros((), piece.dtype), pads)

    return (
        place(before, 0)
        + place(x, before.shape[dim])
        + place(after, before.shape[dim] + x.shape[dim])
    )


def extend(x, depth):
    dim0 = x.ndim - 3
    for axis, dim in (("gx", dim0), ("gy", dim0 + 1)):
        peers = lax.axis_size(axis)
        size = x.shape[dim]
        plan = halo_plan(size, depth)
        if len(plan) > 2:
            whole = lax.all_gather(x, axis, axis=dim, tiled=True)
            pads = [(0, 0, 0)] * x.ndim
            pads[dim] = (depth, depth, 0)
            whole = lax.pad(whole, jnp.zeros((), x.dtype), pads)
            x = lax.dynamic_slice_in_dim(
                whole, lax.axis_index(axis) * size, size + 2 * depth, axis=dim
            )
            continue
        cyclic = any(hop > 1 for _, _, hop in plan)
        for held, take, hop in plan:
            low = lax.slice_in_dim(x, hop * size - take, hop * size, axis=dim)
            start = size + 2 * held - hop * size
            high = lax.slice_in_dim(x, start, start + take, axis=dim)
            if cyclic:
                up = [(i, (i + hop) % peers) for i in range(peers)]
                down = [(i, (i - hop) % peers) for i in range(peers)]
            else:
                up = [(i, i + hop) for i in range(peers - hop)]
                down = [(i + hop, i) for i in range(peers - hop)]
            before = lax.ppermute(low, axis, up)
            after = lax.ppermute(high, axis, down)
            x = join(before, x, after, dim)
        if cyclic:
            index = lax.axis_index(axis) * size + jnp.arange(size + 2 * depth) - depth
            keep = (index >= 0) & (index < size * peers)
            keep = keep.reshape([-1 if d == dim else 1 for d in range(x.ndim)])
            x = jnp.where(keep, x, jnp.zeros_like(x))
    return x


def crop(x, k):
    if k == 0:
        return x
    return x[..., k:-k, k:-k, :]


def neighbours(u):
    centre = u[1:-1, 1:-1]
    zero = jnp.zeros_like(centre[:, :, :1])
    return centre, [
        u[2:, 1:-1],
        u[:-2, 1:-1],
        u[1:-1, 2:],
        u[1:-1, :-2],
        jnp.concatenate([centre[:, :, 1:], zero], axis=2),
        jnp.concatenate([zero, centre[:, :, :-1]], axis=2),
    ]


def pool_matrix(n, dtype):
    rows = jnp.arange(n)[:, None] // 2
    cols = jnp.arange(n // 2)[None, :]
    return (rows == cols).astype(dtype)


def restrict(values):
    first, second, third = values.shape
    pairs = values.reshape(first // 2, 2, second, third)
    summed = pairs[:, 0] + pairs[:, 1]
    pool1 = pool_matrix(second, values.dtype)
    pool2 = pool_matrix(third, values.dtype)
    summed = jnp.einsum("ajk,jb->abk", summed, pool1, precision=lax.Precision.HIGHEST)
    summed = jnp.einsum("abk,kc->abc", summed, pool2, precision=lax.Precision.HIGHEST)
    return summed * 0.125


def prolong(values):
    first, second, third = values.shape
    doubled = jnp.broadcast_to(values[:, None], (first, 2, second, third))
    doubled = doubled.reshape(2 * first, second, third)
    spread1 = pool_matrix(2 * second, values.dtype).T
    spread2 = pool_matrix(2 * third, values.dtype).T
    doubled = jnp.einsum("ajk,jb->abk", doubled, spread1, precision=lax.Precision.HIGHEST)
    return jnp.einsum("abk,kc->abc", doubled, spread2, precision=lax.Precision.HIGHEST)


def inside_mask(shape, depth):
    n0, n1 = shape[0], shape[1]
    rows = lax.axis_index("gx") * n0 + jnp.arange(n0 + 2 * depth) - depth
    cols = lax.axis_index("gy") * n1 + jnp.arange(n1 + 2 * depth) - depth
    ok0 = (rows >= 0) & (rows < n0 * lax.axis_size("gx"))
    ok1 = (cols >= 0) & (cols < n1 * lax.axis_size("gy"))
    return ok0[:, None, None] & ok1[None, :, None]


class Level:
    def __init__(self, source, alpha, beta, inv_spacing, upper, depth):
        self.depth = depth
        stacked = extend(jnp.stack([source, beta, alpha]), self.depth)
        self.source = stacked[0]
        beta_ext = stacked[1]
        self.alpha = stacked[2]
        centre, near = neighbours(beta_ext)
        self.sums = [centre + b for b in near]
        self.mask = inside_mask(source.shape, self.depth)
        self.inv_spacing = inv_spacing
        self.upper = upper

    def apply(self, u, e):
        centre, near = neighbours(u)
        sums = [crop(s, self.depth - e) for s in self.sums]
        alpha = crop(self.alpha, self.depth - e + 1)
        summed = jnp.zeros_like(centre)
        for near_u, near_b in zip(near, sums):
            summed = summed + near_b * (centre - near_u)
        return HELM_SHIFT * alpha * centre + 0.5 * self.inv_spacing * summed

    def residual(self, u, e):
        out = e - 1
        r = crop(self.source, self.depth - out) - self.apply(u, e)
        if out > 0:
            r = jnp.where(crop(self.mask, self.depth - out), r, 0.0)
        return r


def smooth(level, field, e, sweeps, start_zero):
    upper = level.upper
    lower = LOW_FRACTION * upper
    middle = 0.5 * (upper + lower)
    half_width = 0.5 * (upper - lower)
    scaled = middle / half_width
    factor = 1.0 / scaled
    if start_zero:
        e = level.depth
        direction = level.source / middle
        field = direction
    else:
        residual = level.residual(field, e)
        e -= 1
        direction = residual / middle
        field = crop(field, 1) + direction
    for k in range(1, sweeps):
        residual = level.residual(field, e)
        e -= 1
        factor_new = 1.0 / (2.0 * scaled - factor)
        direction = (
            factor_new * factor * crop(direction, 1) + 2.0 * factor_new / half_width * residual
        )
        field = crop(field, 1) + direction
        factor = factor_new
    return field, e


def all_max(values):
    for axis in ("gx", "gy"):
        peers = lax.axis_size(axis)
        if axis == "gy":
            values = jnp.max(lax.all_gather(values, axis), axis=0)
            continue
        if peers & (peers - 1):
            values = lax.pmax(values, axis)
            continue
        step = 1
        while step < peers:
            pairs = [(i, i ^ step) for i in range(peers)]
            values = jnp.maximum(values, lax.ppermute(values, axis, pairs))
            step *= 2
    return values


def local(rhs_field, alpha_coef, beta_coef):
    alphas = [alpha_coef]
    betas = [beta_coef]
    for level_idx in range(1, LEVELS):
        alphas.append(restrict(alphas[-1]))
        betas.append(restrict(betas[-1]))
    maxima = jnp.stack([jnp.stack([jnp.max(alphas[i]), jnp.max(betas[i])]) for i in range(LEVELS)])
    maxima = all_max(maxima)
    uppers = [HELM_SHIFT * maxima[i, 0] + 12.0 * maxima[i, 1] / 4.0**i for i in range(LEVELS)]
    out_depth = [0]
    for level_idx in range(1, LEVELS):
        out_depth.append(-(-(out_depth[-1] + POST_STEPS) // 2))
    depths = [out_depth[i] + POST_STEPS + PRE_STEPS - 1 for i in range(LEVELS - 1)]
    depths.append(out_depth[LEVELS - 1] + COARSE_STEPS - 1)
    levels = []
    fields = []
    source = rhs_field
    for level_idx in range(LEVELS - 1):
        level = Level(
            source,
            alphas[level_idx],
            betas[level_idx],
            1.0 / 4.0**level_idx,
            uppers[level_idx],
            depths[level_idx],
        )
        levels.append(level)
        smoothed, e = smooth(level, None, 0, PRE_STEPS, True)
        residual = level.residual(smoothed, e)
        source = restrict(crop(residual, e - 1))
        fields.append((smoothed, e))
    last = LEVELS - 1
    level = Level(source, alphas[last], betas[last], 1.0 / 4.0**last, uppers[last], depths[last])
    coarse, e = smooth(level, None, 0, COARSE_STEPS, True)
    for level_idx in range(LEVELS - 2, -1, -1):
        smoothed, have = fields[level_idx]
        need = out_depth[level_idx] + POST_STEPS
        correction = crop(prolong(coarse), 2 * e - need)
        coarse, e = smooth(
            levels[level_idx], crop(smoothed, have - need) + correction, need, POST_STEPS, False
        )
    return crop(coarse, e)


def solution(mesh):
    placed = (P("gx", "gy", None), P("gx", "gy", None), P("gx", "gy", None))
    return jax.shard_map(
        local, mesh=mesh, in_specs=placed, out_specs=P("gx", "gy", None), check_vma=False
    )
```

```python
import jax
import jax.numpy as jnp
from jax import lax
from jax.sharding import PartitionSpec as P

LEVELS = 4
PRE_STEPS = 3
POST_STEPS = 3
COARSE_STEPS = 8


HELM_SHIFT = 0.05
LOW_FRACTION = 0.1


def halo_plan(size, depth):
    plan, held = [], 0
    while held < depth:
        take = min(depth - held, (1 + (2 * held) // size) * size)
        hop = -(-take // size)
        plan.append((held, take, hop))
        held += take
    return plan


def join(before, x, after, dim):
    if dim < x.ndim - 2:
        return jnp.concatenate([before, x, after], axis=dim)
    wide = before.shape[dim] + x.shape[dim] + after.shape[dim]

    def place(piece, at):
        pads = [(0, 0, 0)] * x.ndim
        pads[dim] = (at, wide - at - piece.shape[dim], 0)
        return lax.pad(piece, jnp.zeros((), piece.dtype), pads)

    return (
        place(before, 0)
        + place(x, before.shape[dim])
        + place(after, before.shape[dim] + x.shape[dim])
    )


def extend(x, depth):
    dim0 = x.ndim - 3
    for axis, dim in (("gx", dim0), ("gy", dim0 + 1)):
        peers = lax.axis_size(axis)
        size = x.shape[dim]
        plan = halo_plan(size, depth)
        if len(plan) > 2:
            whole = lax.all_gather(x, axis, axis=dim, tiled=True)
            pads = [(0, 0, 0)] * x.ndim
            pads[dim] = (depth, depth, 0)
            whole = lax.pad(whole, jnp.zeros((), x.dtype), pads)
            x = lax.dynamic_slice_in_dim(
                whole, lax.axis_index(axis) * size, size + 2 * depth, axis=dim
            )
            continue
        cyclic = any(hop > 1 for _, _, hop in plan)
        for held, take, hop in plan:
            low = lax.slice_in_dim(x, hop * size - take, hop * size, axis=dim)
            start = size + 2 * held - hop * size
            high = lax.slice_in_dim(x, start, start + take, axis=dim)
            if cyclic:
                up = [(i, (i + hop) % peers) for i in range(peers)]
                down = [(i, (i - hop) % peers) for i in range(peers)]
            else:
                up = [(i, i + hop) for i in range(peers - hop)]
                down = [(i + hop, i) for i in range(peers - hop)]
            before = lax.ppermute(low, axis, up)
            after = lax.ppermute(high, axis, down)
            x = join(before, x, after, dim)
        if cyclic:
            index = lax.axis_index(axis) * size + jnp.arange(size + 2 * depth) - depth
            keep = (index >= 0) & (index < size * peers)
            keep = keep.reshape([-1 if d == dim else 1 for d in range(x.ndim)])
            x = jnp.where(keep, x, jnp.zeros_like(x))
    return x


def crop(x, k):
    if k == 0:
        return x
    return x[..., k:-k, k:-k, :]


def neighbours(u):
    centre = u[1:-1, 1:-1]
    zero = jnp.zeros_like(centre[:, :, :1])
    return centre, [
        u[2:, 1:-1],
        u[:-2, 1:-1],
        u[1:-1, 2:],
        u[1:-1, :-2],
        jnp.concatenate([centre[:, :, 1:], zero], axis=2),
        jnp.concatenate([zero, centre[:, :, :-1]], axis=2),
    ]


def pool_matrix(n, dtype):
    rows = jnp.arange(n)[:, None] // 2
    cols = jnp.arange(n // 2)[None, :]
    return (rows == cols).astype(dtype)


def restrict(values):
    first, second, third = values.shape
    pairs = values.reshape(first // 2, 2, second, third)
    summed = pairs[:, 0] + pairs[:, 1]
    pool1 = pool_matrix(second, values.dtype)
    pool2 = pool_matrix(third, values.dtype)
    summed = jnp.einsum("ajk,jb->abk", summed, pool1, precision=lax.Precision.HIGHEST)
    summed = jnp.einsum("abk,kc->abc", summed, pool2, precision=lax.Precision.HIGHEST)
    return summed * 0.125


def prolong(values):
    first, second, third = values.shape
    doubled = jnp.broadcast_to(values[:, None], (first, 2, second, third))
    doubled = doubled.reshape(2 * first, second, third)
    spread1 = pool_matrix(2 * second, values.dtype).T
    spread2 = pool_matrix(2 * third, values.dtype).T
    doubled = jnp.einsum("ajk,jb->abk", doubled, spread1, precision=lax.Precision.HIGHEST)
    return jnp.einsum("abk,kc->abc", doubled, spread2, precision=lax.Precision.HIGHEST)


def inside_mask(shape, depth):
    n0, n1 = shape[0], shape[1]
    rows = lax.axis_index("gx") * n0 + jnp.arange(n0 + 2 * depth) - depth
    cols = lax.axis_index("gy") * n1 + jnp.arange(n1 + 2 * depth) - depth
    ok0 = (rows >= 0) & (rows < n0 * lax.axis_size("gx"))
    ok1 = (cols >= 0) & (cols < n1 * lax.axis_size("gy"))
    return ok0[:, None, None] & ok1[None, :, None]


class Level:
    def __init__(self, source, alpha, beta, inv_spacing, upper, depth, extended=False):
        self.depth = depth
        if not extended:
            stacked = extend(jnp.stack([source, beta, alpha]), self.depth)
            source, beta, alpha = stacked[0], stacked[1], stacked[2]
        self.source = source
        self.beta = beta
        self.alpha = alpha
        centre, near = neighbours(beta)
        self.sums = [centre + b for b in near]
        n0 = source.shape[0] - 2 * depth
        n1 = source.shape[1] - 2 * depth
        self.mask = inside_mask((n0, n1), self.depth)
        self.inv_spacing = inv_spacing
        self.upper = upper

    def apply(self, u, e):
        centre, near = neighbours(u)
        sums = [crop(s, self.depth - e) for s in self.sums]
        alpha = crop(self.alpha, self.depth - e + 1)
        summed = jnp.zeros_like(centre)
        for near_u, near_b in zip(near, sums):
            summed = summed + near_b * (centre - near_u)
        return HELM_SHIFT * alpha * centre + 0.5 * self.inv_spacing * summed

    def residual(self, u, e):
        out = e - 1
        r = crop(self.source, self.depth - out) - self.apply(u, e)
        if out > 0:
            r = jnp.where(crop(self.mask, self.depth - out), r, 0.0)
        return r


def smooth(level, field, e, sweeps, start_zero):
    upper = level.upper
    lower = LOW_FRACTION * upper
    middle = 0.5 * (upper + lower)
    half_width = 0.5 * (upper - lower)
    scaled = middle / half_width
    factor = 1.0 / scaled
    if start_zero:
        e = level.depth
        direction = level.source / middle
        field = direction
    else:
        residual = level.residual(field, e)
        e -= 1
        direction = residual / middle
        field = crop(field, 1) + direction
    for k in range(1, sweeps):
        residual = level.residual(field, e)
        e -= 1
        factor_new = 1.0 / (2.0 * scaled - factor)
        direction = (
            factor_new * factor * crop(direction, 1) + 2.0 * factor_new / half_width * residual
        )
        field = crop(field, 1) + direction
        factor = factor_new
    return field, e


def all_max(values):
    for axis in ("gx", "gy"):
        peers = lax.axis_size(axis)
        if axis == "gy":
            values = jnp.max(lax.all_gather(values, axis), axis=0)
            continue
        if peers & (peers - 1):
            values = lax.pmax(values, axis)
            continue
        step = 1
        while step < peers:
            pairs = [(i, i ^ step) for i in range(peers)]
            values = jnp.maximum(values, lax.ppermute(values, axis, pairs))
            step *= 2
    return values


def local(rhs_field, alpha_coef, beta_coef):
    alphas = [alpha_coef]
    betas = [beta_coef]
    for level_idx in range(1, LEVELS):
        alphas.append(restrict(alphas[-1]))
        betas.append(restrict(betas[-1]))
    maxima = jnp.stack([jnp.stack([jnp.max(alphas[i]), jnp.max(betas[i])]) for i in range(LEVELS)])
    maxima = all_max(maxima)
    uppers = [HELM_SHIFT * maxima[i, 0] + 12.0 * maxima[i, 1] / 4.0**i for i in range(LEVELS)]
    out_depth = [0]
    for level_idx in range(1, LEVELS):
        out_depth.append(-(-(out_depth[-1] + POST_STEPS) // 2))
    depths = [out_depth[i] + POST_STEPS + PRE_STEPS - 1 for i in range(LEVELS - 1)]
    depths.append(out_depth[LEVELS - 1] + COARSE_STEPS - 1)
    second = LEVELS - 2
    depths[second] = max(depths[second], 2 * depths[LEVELS - 1] + PRE_STEPS)
    levels = []
    fields = []
    source = rhs_field
    for level_idx in range(LEVELS - 1):
        level = Level(
            source,
            alphas[level_idx],
            betas[level_idx],
            1.0 / 4.0**level_idx,
            uppers[level_idx],
            depths[level_idx],
        )
        levels.append(level)
        smoothed, e = smooth(level, None, 0, PRE_STEPS, True)
        residual = level.residual(smoothed, e)
        if level_idx == second:
            keep = 2 * depths[LEVELS - 1]
            source = restrict(crop(residual, e - 1 - keep))
            coarse_beta = restrict(crop(level.beta, level.depth - keep))
            coarse_alpha = restrict(crop(level.alpha, level.depth - keep))
        else:
            source = restrict(crop(residual, e - 1))
        fields.append((smoothed, e))
    last = LEVELS - 1
    level = Level(
        source,
        coarse_alpha,
        coarse_beta,
        1.0 / 4.0**last,
        uppers[last],
        depths[last],
        extended=True,
    )
    coarse, e = smooth(level, None, 0, COARSE_STEPS, True)
    for level_idx in range(LEVELS - 2, -1, -1):
        smoothed, have = fields[level_idx]
        need = out_depth[level_idx] + POST_STEPS
        correction = crop(prolong(coarse), 2 * e - need)
        coarse, e = smooth(
            levels[level_idx], crop(smoothed, have - need) + correction, need, POST_STEPS, False
        )
    return crop(coarse, e)


def solution(mesh):
    placed = (P("gx", "gy", None), P("gx", "gy", None), P("gx", "gy", None))
    return jax.shard_map(
        local, mesh=mesh, in_specs=placed, out_specs=P("gx", "gy", None), check_vma=False
    )
```

```python
import jax
import jax.numpy as jnp
from jax import lax
from jax.sharding import PartitionSpec as P

LEVELS = 4
PRE_STEPS = 3
POST_STEPS = 3
COARSE_STEPS = 8


HELM_SHIFT = 0.05
LOW_FRACTION = 0.1


def halo_plan(size, depth):
    plan, held = [], 0
    while held < depth:
        take = min(depth - held, (1 + (2 * held) // size) * size)
        hop = -(-take // size)
        plan.append((held, take, hop))
        held += take
    return plan


def join(before, x, after, dim):
    if dim < x.ndim - 2:
        return jnp.concatenate([before, x, after], axis=dim)
    wide = before.shape[dim] + x.shape[dim] + after.shape[dim]

    def place(piece, at):
        pads = [(0, 0, 0)] * x.ndim
        pads[dim] = (at, wide - at - piece.shape[dim], 0)
        return lax.pad(piece, jnp.zeros((), piece.dtype), pads)

    return (
        place(before, 0)
        + place(x, before.shape[dim])
        + place(after, before.shape[dim] + x.shape[dim])
    )


def extend(x, depth):
    dim0 = x.ndim - 3
    for axis, dim in (("gx", dim0), ("gy", dim0 + 1)):
        peers = lax.axis_size(axis)
        size = x.shape[dim]
        plan = halo_plan(size, depth)
        if len(plan) > 2:
            whole = lax.all_gather(x, axis, axis=dim, tiled=True)
            pads = [(0, 0, 0)] * x.ndim
            pads[dim] = (depth, depth, 0)
            whole = lax.pad(whole, jnp.zeros((), x.dtype), pads)
            x = lax.dynamic_slice_in_dim(
                whole, lax.axis_index(axis) * size, size + 2 * depth, axis=dim
            )
            continue
        cyclic = any(hop > 1 for _, _, hop in plan)
        for held, take, hop in plan:
            low = lax.slice_in_dim(x, hop * size - take, hop * size, axis=dim)
            start = size + 2 * held - hop * size
            high = lax.slice_in_dim(x, start, start + take, axis=dim)
            if cyclic:
                up = [(i, (i + hop) % peers) for i in range(peers)]
                down = [(i, (i - hop) % peers) for i in range(peers)]
            else:
                up = [(i, i + hop) for i in range(peers - hop)]
                down = [(i + hop, i) for i in range(peers - hop)]
            before = lax.ppermute(low, axis, up)
            after = lax.ppermute(high, axis, down)
            x = join(before, x, after, dim)
        if cyclic:
            index = lax.axis_index(axis) * size + jnp.arange(size + 2 * depth) - depth
            keep = (index >= 0) & (index < size * peers)
            keep = keep.reshape([-1 if d == dim else 1 for d in range(x.ndim)])
            x = jnp.where(keep, x, jnp.zeros_like(x))
    return x


def crop(x, k):
    if k == 0:
        return x
    return x[..., k:-k, k:-k, :]


def neighbours(u):
    centre = u[1:-1, 1:-1]
    zero = jnp.zeros_like(centre[:, :, :1])
    return centre, [
        u[2:, 1:-1],
        u[:-2, 1:-1],
        u[1:-1, 2:],
        u[1:-1, :-2],
        jnp.concatenate([centre[:, :, 1:], zero], axis=2),
        jnp.concatenate([zero, centre[:, :, :-1]], axis=2),
    ]


def pool_matrix(n, dtype):
    rows = jnp.arange(n)[:, None] // 2
    cols = jnp.arange(n // 2)[None, :]
    return (rows == cols).astype(dtype)


def restrict(values):
    first, second, third = values.shape
    pairs = values.reshape(first // 2, 2, second, third)
    summed = pairs[:, 0] + pairs[:, 1]
    pool1 = pool_matrix(second, values.dtype)
    pool2 = pool_matrix(third, values.dtype)
    summed = jnp.einsum("ajk,jb->abk", summed, pool1, precision=lax.Precision.HIGHEST)
    summed = jnp.einsum("abk,kc->abc", summed, pool2, precision=lax.Precision.HIGHEST)
    return summed * 0.125


def prolong(values):
    first, second, third = values.shape
    doubled = jnp.broadcast_to(values[:, None], (first, 2, second, third))
    doubled = doubled.reshape(2 * first, second, third)
    spread1 = pool_matrix(2 * second, values.dtype).T
    spread2 = pool_matrix(2 * third, values.dtype).T
    doubled = jnp.einsum("ajk,jb->abk", doubled, spread1, precision=lax.Precision.HIGHEST)
    return jnp.einsum("abk,kc->abc", doubled, spread2, precision=lax.Precision.HIGHEST)


def inside_mask(shape, depth):
    n0, n1 = shape[0], shape[1]
    rows = lax.axis_index("gx") * n0 + jnp.arange(n0 + 2 * depth) - depth
    cols = lax.axis_index("gy") * n1 + jnp.arange(n1 + 2 * depth) - depth
    ok0 = (rows >= 0) & (rows < n0 * lax.axis_size("gx"))
    ok1 = (cols >= 0) & (cols < n1 * lax.axis_size("gy"))
    return ok0[:, None, None] & ok1[None, :, None]


class Level:
    def __init__(self, source, alpha, beta, inv_spacing, upper, depth):
        self.depth = depth
        stacked = extend(jnp.stack([source, beta, alpha]), self.depth)
        self.source = stacked[0]
        beta_ext = stacked[1]
        self.alpha = stacked[2]
        centre, near = neighbours(beta_ext)
        self.sums = [centre + b for b in near]
        self.mask = inside_mask(source.shape, self.depth)
        self.inv_spacing = inv_spacing
        self.upper = upper

    def apply(self, u, e):
        centre, near = neighbours(u)
        sums = [crop(s, self.depth - e) for s in self.sums]
        alpha = crop(self.alpha, self.depth - e + 1)
        summed = jnp.zeros_like(centre)
        for near_u, near_b in zip(near, sums):
            summed = summed + near_b * (centre - near_u)
        return HELM_SHIFT * alpha * centre + 0.5 * self.inv_spacing * summed

    def residual(self, u, e):
        out = e - 1
        r = crop(self.source, self.depth - out) - self.apply(u, e)
        if out > 0:
            r = jnp.where(crop(self.mask, self.depth - out), r, 0.0)
        return r


def smooth(level, field, e, sweeps, start_zero):
    upper = level.upper
    lower = LOW_FRACTION * upper
    middle = 0.5 * (upper + lower)
    half_width = 0.5 * (upper - lower)
    scaled = middle / half_width
    factor = 1.0 / scaled
    if start_zero:
        e = level.depth
        direction = level.source / middle
        field = direction
    else:
        residual = level.residual(field, e)
        e -= 1
        direction = residual / middle
        field = crop(field, 1) + direction
    for k in range(1, sweeps):
        residual = level.residual(field, e)
        e -= 1
        factor_new = 1.0 / (2.0 * scaled - factor)
        direction = (
            factor_new * factor * crop(direction, 1) + 2.0 * factor_new / half_width * residual
        )
        field = crop(field, 1) + direction
        factor = factor_new
    return field, e


def all_max(values):
    for axis in ("gy", "gx"):
        peers = lax.axis_size(axis)
        if axis == "gy":
            values = jnp.max(lax.all_gather(values, axis), axis=0)
            continue
        if peers & (peers - 1):
            values = lax.pmax(values, axis)
            continue
        step = 1
        while step < peers:
            pairs = [(i, i ^ step) for i in range(peers)]
            values = jnp.maximum(values, lax.ppermute(values, axis, pairs))
            step *= 2
    return values


def local(rhs_field, alpha_coef, beta_coef):
    alphas = [alpha_coef]
    betas = [beta_coef]
    for level_idx in range(1, LEVELS):
        alphas.append(restrict(alphas[-1]))
        betas.append(restrict(betas[-1]))
    maxima = jnp.stack([jnp.stack([jnp.max(alphas[i]), jnp.max(betas[i])]) for i in range(LEVELS)])
    maxima = all_max(maxima)
    uppers = [HELM_SHIFT * maxima[i, 0] + 12.0 * maxima[i, 1] / 4.0**i for i in range(LEVELS)]
    out_depth = [0]
    for level_idx in range(1, LEVELS):
        out_depth.append(-(-(out_depth[-1] + POST_STEPS) // 2))
    depths = [out_depth[i] + POST_STEPS + PRE_STEPS - 1 for i in range(LEVELS - 1)]
    depths.append(out_depth[LEVELS - 1] + COARSE_STEPS - 1)
    levels = []
    fields = []
    source = rhs_field
    for level_idx in range(LEVELS - 1):
        level = Level(
            source,
            alphas[level_idx],
            betas[level_idx],
            1.0 / 4.0**level_idx,
            uppers[level_idx],
            depths[level_idx],
        )
        levels.append(level)
        smoothed, e = smooth(level, None, 0, PRE_STEPS, True)
        residual = level.residual(smoothed, e)
        source = restrict(crop(residual, e - 1))
        fields.append((smoothed, e))
    last = LEVELS - 1
    level = Level(source, alphas[last], betas[last], 1.0 / 4.0**last, uppers[last], depths[last])
    coarse, e = smooth(level, None, 0, COARSE_STEPS, True)
    for level_idx in range(LEVELS - 2, -1, -1):
        smoothed, have = fields[level_idx]
        need = out_depth[level_idx] + POST_STEPS
        correction = crop(prolong(coarse), 2 * e - need)
        coarse, e = smooth(
            levels[level_idx], crop(smoothed, have - need) + correction, need, POST_STEPS, False
        )
    return crop(coarse, e)


def solution(mesh):
    placed = (P("gx", "gy", None), P("gx", "gy", None), P("gx", "gy", None))
    return jax.shard_map(
        local, mesh=mesh, in_specs=placed, out_specs=P("gx", "gy", None), check_vma=False
    )
```

```python
import jax
import jax.numpy as jnp
from jax import lax
from jax.sharding import PartitionSpec as P


LEVELS = 4
PRE_STEPS = 3
POST_STEPS = 3
COARSE_STEPS = 8


HELM_SHIFT = 0.05
LOW_FRACTION = 0.1


def halo_plan(size, depth):
    plan, held = [], 0
    while held < depth:
        take = min(depth - held, (1 + (2 * held) // size) * size)
        hop = -(-take // size)
        plan.append((held, take, hop))
        held += take
    return plan


def join(before, x, after, dim):
    if dim < x.ndim - 2:
        return jnp.concatenate([before, x, after], axis=dim)
    wide = before.shape[dim] + x.shape[dim] + after.shape[dim]

    def place(piece, at):
        pads = [(0, 0, 0)] * x.ndim
        pads[dim] = (at, wide - at - piece.shape[dim], 0)
        return lax.pad(piece, jnp.zeros((), piece.dtype), pads)

    return (
        place(before, 0)
        + place(x, before.shape[dim])
        + place(after, before.shape[dim] + x.shape[dim])
    )


def extend(x, depth):
    dim0 = x.ndim - 3
    for axis, dim in (("gx", dim0), ("gy", dim0 + 1)):
        peers = lax.axis_size(axis)
        size = x.shape[dim]
        plan = halo_plan(size, depth)
        if len(plan) > 2:
            whole = lax.all_gather(x, axis, axis=dim, tiled=True)
            pads = [(0, 0, 0)] * x.ndim
            pads[dim] = (depth, depth, 0)
            whole = lax.pad(whole, jnp.zeros((), x.dtype), pads)
            x = lax.dynamic_slice_in_dim(
                whole, lax.axis_index(axis) * size, size + 2 * depth, axis=dim
            )
            continue
        cyclic = any(hop > 1 for _, _, hop in plan)
        for held, take, hop in plan:
            low = lax.slice_in_dim(x, hop * size - take, hop * size, axis=dim)
            start = size + 2 * held - hop * size
            high = lax.slice_in_dim(x, start, start + take, axis=dim)
            if cyclic:
                up = [(i, (i + hop) % peers) for i in range(peers)]
                down = [(i, (i - hop) % peers) for i in range(peers)]
            else:
                up = [(i, i + hop) for i in range(peers - hop)]
                down = [(i + hop, i) for i in range(peers - hop)]
            before = lax.ppermute(low, axis, up)
            after = lax.ppermute(high, axis, down)
            x = join(before, x, after, dim)
        if cyclic:
            index = lax.axis_index(axis) * size + jnp.arange(size + 2 * depth) - depth
            keep = (index >= 0) & (index < size * peers)
            keep = keep.reshape([-1 if d == dim else 1 for d in range(x.ndim)])
            x = jnp.where(keep, x, jnp.zeros_like(x))
    return x


def crop(x, k):
    if k == 0:
        return x
    return x[..., k:-k, k:-k, :]


def neighbours(u):
    centre = u[1:-1, 1:-1]
    zero = jnp.zeros_like(centre[:, :, :1])
    return centre, [
        u[2:, 1:-1],
        u[:-2, 1:-1],
        u[1:-1, 2:],
        u[1:-1, :-2],
        jnp.concatenate([centre[:, :, 1:], zero], axis=2),
        jnp.concatenate([zero, centre[:, :, :-1]], axis=2),
    ]


def pool_matrix(n, dtype):
    rows = jnp.arange(n)[:, None] // 2
    cols = jnp.arange(n // 2)[None, :]
    return (rows == cols).astype(dtype)


def restrict(values):
    first, second, third = values.shape
    pairs = values.reshape(first // 2, 2, second, third)
    summed = pairs[:, 0] + pairs[:, 1]
    pool1 = pool_matrix(second, values.dtype)
    pool2 = pool_matrix(third, values.dtype)
    summed = jnp.einsum("ajk,jb->abk", summed, pool1, precision=lax.Precision.HIGHEST)
    summed = jnp.einsum("abk,kc->abc", summed, pool2, precision=lax.Precision.HIGHEST)
    return summed * 0.125


def prolong(values):
    first, second, third = values.shape
    doubled = jnp.broadcast_to(values[:, None], (first, 2, second, third))
    doubled = doubled.reshape(2 * first, second, third)
    spread1 = pool_matrix(2 * second, values.dtype).T
    spread2 = pool_matrix(2 * third, values.dtype).T
    doubled = jnp.einsum("ajk,jb->abk", doubled, spread1, precision=lax.Precision.HIGHEST)
    return jnp.einsum("abk,kc->abc", doubled, spread2, precision=lax.Precision.HIGHEST)


def inside_mask(shape, depth):
    n0, n1 = shape[0], shape[1]
    rows = lax.axis_index("gx") * n0 + jnp.arange(n0 + 2 * depth) - depth
    cols = lax.axis_index("gy") * n1 + jnp.arange(n1 + 2 * depth) - depth
    ok0 = (rows >= 0) & (rows < n0 * lax.axis_size("gx"))
    ok1 = (cols >= 0) & (cols < n1 * lax.axis_size("gy"))
    return ok0[:, None, None] & ok1[None, :, None]


class Level:
    def __init__(self, source, alpha, beta, inv_spacing, upper, depth):
        self.depth = depth
        stacked = extend(jnp.stack([source, beta, alpha]), self.depth)
        self.source = stacked[0]
        beta_ext = stacked[1]
        self.alpha = stacked[2]
        centre, near = neighbours(beta_ext)
        self.sums = [centre + b for b in near]
        self.mask = inside_mask(source.shape, self.depth)
        self.inv_spacing = inv_spacing
        self.upper = upper

    def apply(self, u, e):
        centre, near = neighbours(u)
        sums = [crop(s, self.depth - e) for s in self.sums]
        alpha = crop(self.alpha, self.depth - e + 1)
        summed = jnp.zeros_like(centre)
        for near_u, near_b in zip(near, sums):
            summed = summed + near_b * (centre - near_u)
        return HELM_SHIFT * alpha * centre + 0.5 * self.inv_spacing * summed

    def residual(self, u, e):
        out = e - 1
        r = crop(self.source, self.depth - out) - self.apply(u, e)
        if out > 0:
            r = jnp.where(crop(self.mask, self.depth - out), r, 0.0)
        return r


def smooth(level, field, e, sweeps, start_zero):
    upper = level.upper
    lower = LOW_FRACTION * upper
    middle = 0.5 * (upper + lower)
    half_width = 0.5 * (upper - lower)
    scaled = middle / half_width
    factor = 1.0 / scaled
    if start_zero:
        e = level.depth
        direction = level.source / middle
        field = direction
    else:
        residual = level.residual(field, e)
        e -= 1
        direction = residual / middle
        field = crop(field, 1) + direction
    for _ in range(1, sweeps):
        residual = level.residual(field, e)
        e -= 1
        factor_new = 1.0 / (2.0 * scaled - factor)
        direction = (
            factor_new * factor * crop(direction, 1) + 2.0 * factor_new / half_width * residual
        )
        field = crop(field, 1) + direction
        factor = factor_new
    return field, e


def all_max(values):
    for axis in ("gy", "gx"):
        peers = lax.axis_size(axis)
        if axis == "gy":
            values = jnp.max(lax.all_gather(values, axis), axis=0)
            continue
        if peers & (peers - 1):
            values = lax.pmax(values, axis)
            continue
        step = 1
        while step < peers:
            pairs = [(i, i ^ step) for i in range(peers)]
            values = jnp.maximum(values, lax.ppermute(values, axis, pairs))
            step *= 2
    return values


def local(rhs_field, alpha_coef, beta_coef):
    alphas = [alpha_coef]
    betas = [beta_coef]
    for _ in range(1, LEVELS):
        alphas.append(restrict(alphas[-1]))
        betas.append(restrict(betas[-1]))
    maxima = jnp.stack([jnp.stack([jnp.max(alphas[i]), jnp.max(betas[i])]) for i in range(LEVELS)])
    maxima = all_max(maxima)
    uppers = [HELM_SHIFT * maxima[i, 0] + 12.0 * maxima[i, 1] / 4.0**i for i in range(LEVELS)]
    out_depth = [0]
    for _ in range(1, LEVELS):
        out_depth.append(-(-(out_depth[-1] + POST_STEPS) // 2))
    depths = [out_depth[i] + POST_STEPS + PRE_STEPS - 1 for i in range(LEVELS - 1)]
    depths.append(out_depth[LEVELS - 1] + COARSE_STEPS - 1)
    levels = []
    fields = []
    source = rhs_field
    for level_idx in range(LEVELS - 1):
        level = Level(
            source,
            alphas[level_idx],
            betas[level_idx],
            1.0 / 4.0**level_idx,
            uppers[level_idx],
            depths[level_idx],
        )
        levels.append(level)
        smoothed, e = smooth(level, None, 0, PRE_STEPS, True)
        residual = level.residual(smoothed, e)
        source = restrict(crop(residual, e - 1))
        fields.append((smoothed, e))
    last = LEVELS - 1
    level = Level(source, alphas[last], betas[last], 1.0 / 4.0**last, uppers[last], depths[last])
    coarse, e = smooth(level, None, 0, COARSE_STEPS, True)
    for level_idx in range(LEVELS - 2, -1, -1):
        smoothed, have = fields[level_idx]
        need = out_depth[level_idx] + POST_STEPS
        correction = crop(prolong(coarse), 2 * e - need)
        coarse, e = smooth(
            levels[level_idx], crop(smoothed, have - need) + correction, need, POST_STEPS, False
        )
    return crop(coarse, e)


def solution(mesh):
    placed = (P("gx", "gy", None), P("gx", "gy", None), P("gx", "gy", None))
    return jax.shard_map(
        local, mesh=mesh, in_specs=placed, out_specs=P("gx", "gy", None), check_vma=False
    )
```

```python
import jax
import jax.numpy as jnp
from jax import lax
from jax.sharding import PartitionSpec as P

LEVELS = 4
PRE_STEPS = 3
POST_STEPS = 3
COARSE_STEPS = 8


HELM_SHIFT = 0.05
LOW_FRACTION = 0.1


def halo_plan(size, depth):
    plan, held = [], 0
    while held < depth:
        take = min(depth - held, (1 + (2 * held) // size) * size)
        hop = -(-take // size)
        plan.append((held, take, hop))
        held += take
    return plan


def join(before, x, after, dim):
    if dim < x.ndim - 2:
        return jnp.concatenate([before, x, after], axis=dim)
    wide = before.shape[dim] + x.shape[dim] + after.shape[dim]

    def place(piece, at):
        pads = [(0, 0, 0)] * x.ndim
        pads[dim] = (at, wide - at - piece.shape[dim], 0)
        return lax.pad(piece, jnp.zeros((), piece.dtype), pads)

    return (
        place(before, 0)
        + place(x, before.shape[dim])
        + place(after, before.shape[dim] + x.shape[dim])
    )


def extend(x, depth):
    dim0 = x.ndim - 3
    for axis, dim in (("gx", dim0), ("gy", dim0 + 1)):
        peers = lax.axis_size(axis)
        size = x.shape[dim]
        plan = halo_plan(size, depth)
        if len(plan) > 2:
            whole = lax.all_gather(x, axis, axis=dim, tiled=True)
            pads = [(0, 0, 0)] * x.ndim
            pads[dim] = (depth, depth, 0)
            whole = lax.pad(whole, jnp.zeros((), x.dtype), pads)
            x = lax.dynamic_slice_in_dim(
                whole, lax.axis_index(axis) * size, size + 2 * depth, axis=dim
            )
            continue
        cyclic = any(hop > 1 for _, _, hop in plan)
        for held, take, hop in plan:
            low = lax.slice_in_dim(x, hop * size - take, hop * size, axis=dim)
            start = size + 2 * held - hop * size
            high = lax.slice_in_dim(x, start, start + take, axis=dim)
            if cyclic:
                up = [(i, (i + hop) % peers) for i in range(peers)]
                down = [(i, (i - hop) % peers) for i in range(peers)]
            else:
                up = [(i, i + hop) for i in range(peers - hop)]
                down = [(i + hop, i) for i in range(peers - hop)]
            before = lax.ppermute(low, axis, up)
            after = lax.ppermute(high, axis, down)
            x = join(before, x, after, dim)
        if cyclic:
            index = lax.axis_index(axis) * size + jnp.arange(size + 2 * depth) - depth
            keep = (index >= 0) & (index < size * peers)
            keep = keep.reshape([-1 if d == dim else 1 for d in range(x.ndim)])
            x = jnp.where(keep, x, jnp.zeros_like(x))
    return x


def crop(x, k):
    if k == 0:
        return x
    return x[..., k:-k, k:-k, :]


def neighbours(u):
    centre = u[1:-1, 1:-1]
    zero = jnp.zeros_like(centre[:, :, :1])
    return centre, [
        u[2:, 1:-1],
        u[:-2, 1:-1],
        u[1:-1, 2:],
        u[1:-1, :-2],
        jnp.concatenate([centre[:, :, 1:], zero], axis=2),
        jnp.concatenate([zero, centre[:, :, :-1]], axis=2),
    ]


def pool_matrix(n, dtype):
    rows = jnp.arange(n)[:, None] // 2
    cols = jnp.arange(n // 2)[None, :]
    return (rows == cols).astype(dtype)


def restrict(values):
    first, second, third = values.shape
    pairs = values.reshape(first // 2, 2, second, third)
    summed = pairs[:, 0] + pairs[:, 1]
    pool1 = pool_matrix(second, values.dtype)
    pool2 = pool_matrix(third, values.dtype)
    summed = jnp.einsum("ajk,jb->abk", summed, pool1, precision=lax.Precision.HIGHEST)
    summed = jnp.einsum("abk,kc->abc", summed, pool2, precision=lax.Precision.HIGHEST)
    return summed * 0.125


def prolong(values):
    first, second, third = values.shape
    doubled = jnp.broadcast_to(values[:, None], (first, 2, second, third))
    doubled = doubled.reshape(2 * first, second, third)
    spread1 = pool_matrix(2 * second, values.dtype).T
    spread2 = pool_matrix(2 * third, values.dtype).T
    doubled = jnp.einsum("ajk,jb->abk", doubled, spread1, precision=lax.Precision.HIGHEST)
    return jnp.einsum("abk,kc->abc", doubled, spread2, precision=lax.Precision.HIGHEST)


def inside_mask(shape, depth):
    n0, n1 = shape[0], shape[1]
    rows = lax.axis_index("gx") * n0 + jnp.arange(n0 + 2 * depth) - depth
    cols = lax.axis_index("gy") * n1 + jnp.arange(n1 + 2 * depth) - depth
    ok0 = (rows >= 0) & (rows < n0 * lax.axis_size("gx"))
    ok1 = (cols >= 0) & (cols < n1 * lax.axis_size("gy"))
    return ok0[:, None, None] & ok1[None, :, None]


class Level:
    def __init__(self, source, alpha, beta, inv_spacing, upper, depth):
        self.depth = depth
        stacked = extend(jnp.stack([source, beta, alpha]), self.depth)
        self.source = stacked[0]
        beta_ext = stacked[1]
        self.alpha = stacked[2]
        centre, near = neighbours(beta_ext)
        self.sums = [centre + b for b in near]
        self.mask = inside_mask(source.shape, self.depth)
        self.inv_spacing = inv_spacing
        self.upper = upper

    def apply(self, u, e):
        centre, near = neighbours(u)
        sums = [crop(s, self.depth - e) for s in self.sums]
        alpha = crop(self.alpha, self.depth - e + 1)
        summed = jnp.zeros_like(centre)
        for near_u, near_b in zip(near, sums):
            summed = summed + near_b * (centre - near_u)
        return HELM_SHIFT * alpha * centre + 0.5 * self.inv_spacing * summed

    def residual(self, u, e):
        out = e - 1
        r = crop(self.source, self.depth - out) - self.apply(u, e)
        if out > 0:
            r = jnp.where(crop(self.mask, self.depth - out), r, 0.0)
        return r


def smooth(level, field, e, sweeps, start_zero):
    upper = level.upper
    lower = LOW_FRACTION * upper
    middle = 0.5 * (upper + lower)
    half_width = 0.5 * (upper - lower)
    scaled = middle / half_width
    factor = 1.0 / scaled
    if start_zero:
        e = level.depth
        direction = level.source / middle
        field = direction
    else:
        residual = level.residual(field, e)
        e -= 1
        direction = residual / middle
        field = crop(field, 1) + direction
    for k in range(1, sweeps):
        residual = level.residual(field, e)
        e -= 1
        factor_new = 1.0 / (2.0 * scaled - factor)
        direction = (
            factor_new * factor * crop(direction, 1) + 2.0 * factor_new / half_width * residual
        )
        field = crop(field, 1) + direction
        factor = factor_new
    return field, e


def all_max(values):
    for axis in ("gy", "gx"):
        peers = lax.axis_size(axis)
        if axis == "gy":
            values = jnp.max(lax.all_gather(values, axis), axis=0)
            continue
        if peers & (peers - 1):
            values = lax.pmax(values, axis)
            continue
        step = peers // 2
        while step >= 1:
            pairs = [(i, i ^ step) for i in range(peers)]
            values = jnp.maximum(values, lax.ppermute(values, axis, pairs))
            step //= 2
    return values


def local(rhs_field, alpha_coef, beta_coef):
    alphas = [alpha_coef]
    betas = [beta_coef]
    for level_idx in range(1, LEVELS):
        alphas.append(restrict(alphas[-1]))
        betas.append(restrict(betas[-1]))
    maxima = jnp.stack([jnp.stack([jnp.max(alphas[i]), jnp.max(betas[i])]) for i in range(LEVELS)])
    maxima = all_max(maxima)
    uppers = [HELM_SHIFT * maxima[i, 0] + 12.0 * maxima[i, 1] / 4.0**i for i in range(LEVELS)]
    out_depth = [0]
    for level_idx in range(1, LEVELS):
        out_depth.append(-(-(out_depth[-1] + POST_STEPS) // 2))
    depths = [out_depth[i] + POST_STEPS + PRE_STEPS - 1 for i in range(LEVELS - 1)]
    depths.append(out_depth[LEVELS - 1] + COARSE_STEPS - 1)
    levels = []
    fields = []
    source = rhs_field
    for level_idx in range(LEVELS - 1):
        level = Level(
            source,
            alphas[level_idx],
            betas[level_idx],
            1.0 / 4.0**level_idx,
            uppers[level_idx],
            depths[level_idx],
        )
        levels.append(level)
        smoothed, e = smooth(level, None, 0, PRE_STEPS, True)
        residual = level.residual(smoothed, e)
        source = restrict(crop(residual, e - 1))
        fields.append((smoothed, e))
    last = LEVELS - 1
    level = Level(source, alphas[last], betas[last], 1.0 / 4.0**last, uppers[last], depths[last])
    coarse, e = smooth(level, None, 0, COARSE_STEPS, True)
    for level_idx in range(LEVELS - 2, -1, -1):
        smoothed, have = fields[level_idx]
        need = out_depth[level_idx] + POST_STEPS
        correction = crop(prolong(coarse), 2 * e - need)
        coarse, e = smooth(
            levels[level_idx], crop(smoothed, have - need) + correction, need, POST_STEPS, False
        )
    return crop(coarse, e)


def solution(mesh):
    placed = (P("gx", "gy", None), P("gx", "gy", None), P("gx", "gy", None))
    return jax.shard_map(
        local, mesh=mesh, in_specs=placed, out_specs=P("gx", "gy", None), check_vma=False
    )
```

```python
import jax
import jax.numpy as jnp
from jax import lax
from jax.sharding import PartitionSpec as P

LEVELS = 4
PRE_STEPS = 3
POST_STEPS = 3
COARSE_STEPS = 8


HELM_SHIFT = 0.05
LOW_FRACTION = 0.1


def halo_plan(size, depth):
    plan, held = [], 0
    while held < depth:
        take = min(depth - held, (1 + (2 * held) // size) * size)
        hop = -(-take // size)
        plan.append((held, take, hop))
        held += take
    return plan


def join(before, x, after, dim):
    if dim < x.ndim - 2:
        return jnp.concatenate([before, x, after], axis=dim)
    wide = before.shape[dim] + x.shape[dim] + after.shape[dim]

    def place(piece, at):
        pads = [(0, 0, 0)] * x.ndim
        pads[dim] = (at, wide - at - piece.shape[dim], 0)
        return lax.pad(piece, jnp.zeros((), piece.dtype), pads)

    return (
        place(before, 0)
        + place(x, before.shape[dim])
        + place(after, before.shape[dim] + x.shape[dim])
    )


def extend(x, depth):
    dim0 = x.ndim - 3
    for axis, dim in (("gx", dim0), ("gy", dim0 + 1)):
        peers = lax.axis_size(axis)
        size = x.shape[dim]
        plan = halo_plan(size, depth)
        if len(plan) > 2:
            whole = lax.all_gather(x, axis, axis=dim, tiled=True)
            pads = [(0, 0, 0)] * x.ndim
            pads[dim] = (depth, depth, 0)
            whole = lax.pad(whole, jnp.zeros((), x.dtype), pads)
            x = lax.dynamic_slice_in_dim(
                whole, lax.axis_index(axis) * size, size + 2 * depth, axis=dim
            )
            continue
        cyclic = any(hop > 1 for _, _, hop in plan)
        for held, take, hop in plan:
            low = lax.slice_in_dim(x, hop * size - take, hop * size, axis=dim)
            start = size + 2 * held - hop * size
            high = lax.slice_in_dim(x, start, start + take, axis=dim)
            if cyclic:
                up = [(i, (i + hop) % peers) for i in range(peers)]
                down = [(i, (i - hop) % peers) for i in range(peers)]
            else:
                up = [(i, i + hop) for i in range(peers - hop)]
                down = [(i + hop, i) for i in range(peers - hop)]
            before = lax.ppermute(low, axis, up)
            after = lax.ppermute(high, axis, down)
            x = join(before, x, after, dim)
        if cyclic:
            index = lax.axis_index(axis) * size + jnp.arange(size + 2 * depth) - depth
            keep = (index >= 0) & (index < size * peers)
            keep = keep.reshape([-1 if d == dim else 1 for d in range(x.ndim)])
            x = jnp.where(keep, x, jnp.zeros_like(x))
    return x


def crop(x, k):
    if k == 0:
        return x
    return x[..., k:-k, k:-k, :]


def neighbours(u):
    centre = u[1:-1, 1:-1]
    zero = jnp.zeros_like(centre[:, :, :1])
    return centre, [
        u[2:, 1:-1],
        u[:-2, 1:-1],
        u[1:-1, 2:],
        u[1:-1, :-2],
        jnp.concatenate([centre[:, :, 1:], zero], axis=2),
        jnp.concatenate([zero, centre[:, :, :-1]], axis=2),
    ]


def pool_matrix(n, dtype):
    rows = jnp.arange(n)[:, None] // 2
    cols = jnp.arange(n // 2)[None, :]
    return (rows == cols).astype(dtype)


def restrict(values):
    first, second, third = values.shape
    pairs = values.reshape(first // 2, 2, second, third)
    summed = pairs[:, 0] + pairs[:, 1]
    pool1 = pool_matrix(second, values.dtype)
    pool2 = pool_matrix(third, values.dtype)
    summed = jnp.einsum("ajk,jb->abk", summed, pool1, precision=lax.Precision.HIGHEST)
    summed = jnp.einsum("abk,kc->abc", summed, pool2, precision=lax.Precision.HIGHEST)
    return summed * 0.125


def prolong(values):
    first, second, third = values.shape
    doubled = jnp.broadcast_to(values[:, None], (first, 2, second, third))
    doubled = doubled.reshape(2 * first, second, third)
    spread1 = pool_matrix(2 * second, values.dtype).T
    spread2 = pool_matrix(2 * third, values.dtype).T
    doubled = jnp.einsum("ajk,jb->abk", doubled, spread1, precision=lax.Precision.HIGHEST)
    return jnp.einsum("abk,kc->abc", doubled, spread2, precision=lax.Precision.HIGHEST)


def inside_mask(shape, depth):
    n0, n1 = shape[0], shape[1]
    rows = lax.axis_index("gx") * n0 + jnp.arange(n0 + 2 * depth) - depth
    cols = lax.axis_index("gy") * n1 + jnp.arange(n1 + 2 * depth) - depth
    ok0 = (rows >= 0) & (rows < n0 * lax.axis_size("gx"))
    ok1 = (cols >= 0) & (cols < n1 * lax.axis_size("gy"))
    return ok0[:, None, None] & ok1[None, :, None]


class Level:
    def __init__(self, source, alpha, beta, inv_spacing, upper, depth):
        self.depth = depth
        stacked = extend(jnp.stack([source, beta, alpha]), self.depth)
        self.source = stacked[0]
        beta_ext = stacked[1]
        self.alpha = stacked[2]
        centre, near = neighbours(beta_ext)
        self.sums = [centre + b for b in near]
        self.mask = inside_mask(source.shape, self.depth)
        self.inv_spacing = inv_spacing
        self.upper = upper

    def apply(self, u, e):
        centre, near = neighbours(u)
        sums = [crop(s, self.depth - e) for s in self.sums]
        alpha = crop(self.alpha, self.depth - e + 1)
        summed = jnp.zeros_like(centre)
        for near_u, near_b in zip(near, sums):
            summed = summed + near_b * (centre - near_u)
        return HELM_SHIFT * alpha * centre + 0.5 * self.inv_spacing * summed

    def residual(self, u, e):
        out = e - 1
        r = crop(self.source, self.depth - out) - self.apply(u, e)
        if out > 0:
            r = jnp.where(crop(self.mask, self.depth - out), r, 0.0)
        return r


def smooth(level, field, e, sweeps, start_zero):
    upper = level.upper
    lower = LOW_FRACTION * upper
    middle = 0.5 * (upper + lower)
    half_width = 0.5 * (upper - lower)
    scaled = middle / half_width
    factor = 1.0 / scaled
    if start_zero:
        e = level.depth
        direction = level.source / middle
        field = direction
    else:
        residual = level.residual(field, e)
        e -= 1
        direction = residual / middle
        field = crop(field, 1) + direction
    for k in range(1, sweeps):
        residual = level.residual(field, e)
        e -= 1
        factor_new = 1.0 / (2.0 * scaled - factor)
        direction = (
            factor_new * factor * crop(direction, 1) + 2.0 * factor_new / half_width * residual
        )
        field = crop(field, 1) + direction
        factor = factor_new
    return field, e


def all_max(values):
    for axis in ("gy", "gx"):
        peers = lax.axis_size(axis)
        if peers & (peers - 1):
            values = lax.pmax(values, axis)
            continue
        step = peers // 2
        while step >= 1:
            pairs = [(i, i ^ step) for i in range(peers)]
            values = jnp.maximum(values, lax.ppermute(values, axis, pairs))
            step //= 2
    return values


def local(rhs_field, alpha_coef, beta_coef):
    alphas = [alpha_coef]
    betas = [beta_coef]
    for level_idx in range(1, LEVELS):
        alphas.append(restrict(alphas[-1]))
        betas.append(restrict(betas[-1]))
    maxima = jnp.stack([jnp.stack([jnp.max(alphas[i]), jnp.max(betas[i])]) for i in range(LEVELS)])
    maxima = all_max(maxima)
    uppers = [HELM_SHIFT * maxima[i, 0] + 12.0 * maxima[i, 1] / 4.0**i for i in range(LEVELS)]
    out_depth = [0]
    for level_idx in range(1, LEVELS):
        out_depth.append(-(-(out_depth[-1] + POST_STEPS) // 2))
    depths = [out_depth[i] + POST_STEPS + PRE_STEPS - 1 for i in range(LEVELS - 1)]
    depths.append(out_depth[LEVELS - 1] + COARSE_STEPS - 1)
    levels = []
    fields = []
    source = rhs_field
    for level_idx in range(LEVELS - 1):
        level = Level(
            source,
            alphas[level_idx],
            betas[level_idx],
            1.0 / 4.0**level_idx,
            uppers[level_idx],
            depths[level_idx],
        )
        levels.append(level)
        smoothed, e = smooth(level, None, 0, PRE_STEPS, True)
        residual = level.residual(smoothed, e)
        source = restrict(crop(residual, e - 1))
        fields.append((smoothed, e))
    last = LEVELS - 1
    level = Level(source, alphas[last], betas[last], 1.0 / 4.0**last, uppers[last], depths[last])
    coarse, e = smooth(level, None, 0, COARSE_STEPS, True)
    for level_idx in range(LEVELS - 2, -1, -1):
        smoothed, have = fields[level_idx]
        need = out_depth[level_idx] + POST_STEPS
        correction = crop(prolong(coarse), 2 * e - need)
        coarse, e = smooth(
            levels[level_idx], crop(smoothed, have - need) + correction, need, POST_STEPS, False
        )
    return crop(coarse, e)


def solution(mesh):
    placed = (P("gx", "gy", None), P("gx", "gy", None), P("gx", "gy", None))
    return jax.shard_map(
        local, mesh=mesh, in_specs=placed, out_specs=P("gx", "gy", None), check_vma=False
    )
```
